32 devices in a mesh: ctx: 8 (over z, x), head: 4 (over y, core).
Axes of the slice: x: 2, y: 2, z: 4, core: 2. Of those that a mesh axis runs over, the one named last changes fastest.
Arguments:
- queries: bfloat16 [4096, 4096], P('ctx', 'head'), may hold values from -6 to 6
- key_states: bfloat16 [4096, 4096], P('ctx', 'head'), may hold values from -6 to 6
- value_states: bfloat16 [4096, 4096], P('ctx', 'head'), may hold values from -6 to 6
- transition_vectors: bfloat16 [4096, 4096], P('ctx', 'head'), may hold values from -6 to 6
- beta_logit: float32 [4096, 32], P('ctx', 'head'), may hold values from -6 to 6
- document_ids: int32 [4096], P('ctx'), may hold values from 0 to 7, as said below
- out_weight: bfloat16 [4096, 4096], P('head'), may hold values from -0.09375 to 0.09375
Outputs:
- layer_out: bfloat16 [4096, 4096], P(('ctx', 'head'))
The draws below stay inside these ranges and needn't reach their ends.
Inputs may be any that keep to these rules, and one draw needn't show every extreme that they name: `document_ids`: document ids never fall along the sequence; document 0 is the first 2304 tokens; the other documents have 1 or more tokens each and together fill the rest.
All inputs are finite; a program needn't handle non-finite values.
Results may differ from the reference program's by a relative error of at most 0.022.
Values may be sent and summed in bfloat16 or wider, within the bound.
No kernel may reach another device: no remote copies, remote signals or barrier semaphores. Data moves between devices by JAX's collectives and lax.ppermute only.
A program may use at most 128 MiB of HBM per device.

```python
import jax
import jax.numpy as jnp
from jax import lax

HEADS = 32
DH = 128
D = 4096
TOK_DEV = 512
TOKENS = 4096
N_CTX = 8


def draw_queries(key, part):
    drawn = jnp.clip(jax.random.normal(jax.random.fold_in(key, 11), (TOKENS, HEADS * DH), jnp.float32), -6.0, 6.0)
    return drawn.astype(jnp.bfloat16)


def draw_key_states(key, part):
    drawn = jnp.clip(jax.random.normal(jax.random.fold_in(key, 12), (TOKENS, HEADS * DH), jnp.float32), -6.0, 6.0)
    return drawn.astype(jnp.bfloat16)


def draw_beta_logit(key, part):
    sign_values = 2.0 * jax.random.randint(jax.random.fold_in(key, 14), (TOKENS, HEADS), 0, 2).astype(jnp.float32) - 1.0
    magnitude = jax.random.uniform(jax.random.fold_in(key, 13), (TOKENS, HEADS), jnp.float32, 4.75, 6.0)
    drawn = sign_values * magnitude
    return drawn.astype(jnp.float32)


def draw_document_ids(key, part):
    first_length = TOKENS // 2 + TOK_DEV // 2
    rest_length = TOKENS - first_length
    seeded = jax.random.fold_in(key, 5209)
    cut_points = jax.random.permutation(seeded, rest_length - 1)[:6].astype(jnp.int32) + 1
    positions = jnp.arange(TOKENS, dtype=jnp.int32)
    offsets = positions - first_length
    later = 1 + jnp.sum((cut_points[None, :] <= offsets[:, None]).astype(jnp.int32), axis=1)
    return jnp.where(positions < first_length, 0, later).astype(jnp.int32)


def block_levels(stream_key, shape, pieces, least, top_value):
    def one(dim, parts):
        draws = jax.random.uniform(jax.random.fold_in(jax.random.fold_in(stream_key, 6), dim), (parts,), jnp.float32, least / len(pieces), top_value / len(pieces))
        return jnp.repeat(jnp.exp(draws), shape[dim] // parts).reshape((-1,) + (1,) * (len(shape) - dim - 1))

    level = one(*pieces[0])
    for cut in pieces[1:]:
        level = level * one(*cut)
    return level


def gaussian(rng, dims, width, bound, split=(), kind=jnp.bfloat16):
    values = width * jax.random.normal(rng, dims, jnp.float32)
    if split:
        values = values * block_levels(rng, dims, split, -0.22, 0.18)
    return jnp.clip(values, -bound, bound).astype(kind)


def setup_inputs(seed: int = 0) -> dict:
    key_list = jax.random.split(jax.random.key(seed), 8)
    queries = draw_queries(jax.random.fold_in(key_list[7], 71), 0)
    key_states = draw_key_states(jax.random.fold_in(key_list[7], 71), 0)
    value_states = gaussian(key_list[2], (TOKENS, D), 1.0, 6.0, ((0, 8), (1, 4)))
    transition_vectors = gaussian(key_list[3], (TOKENS, D), 1.0, 6.0, ((0, 8), (1, 4)))
    beta_logit = draw_beta_logit(jax.random.fold_in(key_list[7], 71), 0)
    document_ids = draw_document_ids(jax.random.fold_in(key_list[7], 71), 0)
    out_weight = gaussian(key_list[6], (D, D), D ** -0.5, 0.09375, ((0, 4),))
    return dict(queries=queries, key_states=key_states, value_states=value_states, transition_vectors=transition_vectors, beta_logit=beta_logit, document_ids=document_ids, out_weight=out_weight)


epsilon = 1e-06
masked_value = -1e+30
highest = lax.Precision.HIGHEST

def shard_operators(query_block, key_block, vector_block, strength):
    block_rows = key_block.shape[0]
    head_width = key_block.shape[1]
    row_ids = jnp.arange(block_rows)
    strict = row_ids[:, None] > row_ids[None, :]
    causal = row_ids[:, None] >= row_ids[None, :]
    intersections = jnp.dot(vector_block, vector_block.T, precision=highest)
    unit_lower = jnp.where(strict, intersections * strength[None, :], 0.0) + jnp.eye(block_rows, dtype=jnp.float32)
    key_proj = jnp.where(strict, jnp.dot(vector_block, key_block.T, precision=highest), 0.0)
    solved = lax.linalg.triangular_solve(unit_lower, jnp.concatenate([key_proj, vector_block], axis=1), left_side=True, lower=True, unit_diagonal=True)
    key_solve = solved[:, :block_rows]
    vector_solve = solved[:, block_rows:]
    weighted = strength[:, None] * vector_block
    keys_end = (key_block - jnp.dot(key_solve.T, weighted, precision=highest)).astype(jnp.bfloat16)
    transfer = jnp.eye(head_width, dtype=jnp.float32) - jnp.dot(vector_block.T, strength[:, None] * vector_solve, precision=highest)
    query_dots = jnp.where(causal, jnp.dot(query_block, vector_block.T, precision=highest), 0.0)
    scaled_dots = query_dots * strength[None, :]
    intra_scores = jnp.dot(query_block, key_block.T, precision=highest) - jnp.dot(scaled_dots, key_solve, precision=highest)
    rotated = query_block - jnp.dot(scaled_dots, vector_solve, precision=highest)
    return (intra_scores, keys_end, transfer, rotated)

def one_head(operands, document_ids):
    query_head, key_head, value_head, vector_head, logit_head = operands
    block_rows = TOK_DEV
    head_width = query_head.shape[1]
    score_scale = head_width ** (-0.5)
    strength = 2.0 * jax.nn.sigmoid(logit_head)
    vector_float = vector_head.astype(jnp.float32)
    unit_vectors = vector_float / jnp.sqrt(lax.optimization_barrier(jnp.sum(vector_float * vector_float, axis=1, keepdims=True)) + epsilon)
    row_ids = jnp.arange(block_rows)
    causal = row_ids[:, None] >= row_ids[None, :]
    operators = []
    for anchor in range(N_CTX):
        lower_end = anchor * block_rows
        upper_end = lower_end + block_rows
        operators.append(shard_operators(query_head[lower_end:upper_end].astype(jnp.float32), key_head[lower_end:upper_end].astype(jnp.float32), unit_vectors[lower_end:upper_end], strength[lower_end:upper_end]))
    results = []
    for target in range(N_CTX):
        query_docs = document_ids[target * block_rows:(target + 1) * block_rows]
        intra_scores, keys_end, transfer, rotated = operators[target]
        allowed = causal & (query_docs[:, None] == query_docs[None, :])
        blocks = [jnp.where(allowed, intra_scores * score_scale, masked_value)]
        value_parts = [value_head[target * block_rows:(target + 1) * block_rows]]
        for anchor in range(target - 1, -1, -1):
            key_docs = document_ids[anchor * block_rows:(anchor + 1) * block_rows]
            scores = jnp.dot(rotated.astype(jnp.bfloat16).astype(jnp.float32), operators[anchor][1].T.astype(jnp.float32), preferred_element_type=jnp.float32)
            blocks.append(jnp.where(query_docs[:, None] == key_docs[None, :], scores * score_scale, masked_value))
            value_parts.append(value_head[anchor * block_rows:(anchor + 1) * block_rows])
            rotated = jnp.dot(rotated, operators[anchor][2], precision=highest)
        scores = jnp.concatenate(blocks, axis=1)
        row_max = lax.optimization_barrier(jnp.max(scores, axis=1, keepdims=True))
        weights = jnp.exp(scores - row_max)
        row_total = lax.optimization_barrier(jnp.sum(weights, axis=1, keepdims=True))
        mixed = jnp.dot(weights.astype(jnp.bfloat16).astype(jnp.float32), jnp.concatenate(value_parts, axis=0).astype(jnp.float32), preferred_element_type=jnp.float32)
        results.append((mixed / row_total).astype(jnp.bfloat16))
    return jnp.concatenate(results, axis=0)

def reference(queries, key_states, value_states, transition_vectors, beta_logit, document_ids, out_weight):

    def split_heads(flat):
        return jnp.transpose(flat.reshape(TOKENS, HEADS, DH), (1, 0, 2))
    per_head = lax.map(lambda operands: one_head(operands, document_ids), (split_heads(queries), split_heads(key_states), split_heads(value_states), split_heads(transition_vectors), beta_logit.T))
    attended = jnp.transpose(per_head, (1, 0, 2)).reshape(TOKENS, HEADS * DH)
    return jnp.dot(attended.astype(jnp.float32), out_weight.astype(jnp.float32), preferred_element_type=jnp.float32).astype(jnp.bfloat16)
```

```python
import jax
import jax.numpy as jnp
from jax import lax
from jax.sharding import PartitionSpec as P

epsilon = 1e-06
masked_value = -1e30
highest = lax.Precision.HIGHEST


def diagonal_blocks(matrix, size):
    count = matrix.shape[0] // size
    tiled = matrix.reshape(count, size, count, size)
    mask = jnp.eye(count, dtype=bool)[:, None, :, None]
    return jnp.sum(jnp.where(mask, tiled, 0.0), axis=2)


def unit_lower_inverse(strict_lower):
    rows_total = strict_lower.shape[0]
    leaf = 16
    leaves = diagonal_blocks(strict_lower, leaf)
    rows = []
    for i in range(leaf):
        row = jnp.broadcast_to((jnp.arange(leaf) == i).astype(jnp.float32), leaves.shape[:1] + (leaf,))
        for m in range(i):
            row = row - leaves[:, i, m][:, None] * rows[m]
        rows.append(row)
    inverse = jnp.stack(rows, axis=1)
    size = leaf
    while size < rows_total:
        pairs = rows_total // (2 * size)
        lower = diagonal_blocks(strict_lower, 2 * size)[:, size:, :size]
        halves = inverse.reshape(pairs, 2, size, size)
        first = halves[:, 0]
        second = halves[:, 1]
        corner = -jnp.einsum(
            "pij,pjk->pik",
            second,
            jnp.einsum("pij,pjk->pik", lower, first, precision=highest),
            precision=highest,
        )
        top = jnp.concatenate([first, jnp.zeros_like(first)], axis=2)
        bottom = jnp.concatenate([corner, second], axis=2)
        inverse = jnp.concatenate([top, bottom], axis=1)
        size *= 2
    return inverse[0]


def lower_solve(strict_lower, right):
    rows_total = strict_lower.shape[0]
    leaf = 16
    count = rows_total // leaf
    if rows_total % leaf or count & (count - 1):
        unit_lower = strict_lower + jnp.eye(rows_total, dtype=jnp.float32)
        return lax.linalg.triangular_solve(
            unit_lower, right, left_side=True, lower=True, unit_diagonal=True
        )
    return jnp.dot(unit_lower_inverse(strict_lower), right, precision=highest)


def shard_operators(query_block, key_block, vector_block, strength):
    block_rows = key_block.shape[0]
    head_width = key_block.shape[1]
    row_ids = jnp.arange(block_rows)
    strict = row_ids[:, None] > row_ids[None, :]
    causal = row_ids[:, None] >= row_ids[None, :]
    intersections = jnp.dot(vector_block, vector_block.T, precision=highest)
    strict_lower = jnp.where(strict, intersections * strength[None, :], 0.0)
    key_proj = jnp.where(strict, jnp.dot(vector_block, key_block.T, precision=highest), 0.0)
    solved = lower_solve(strict_lower, jnp.concatenate([key_proj, vector_block], axis=1))
    key_solve = solved[:, :block_rows]
    vector_solve = solved[:, block_rows:]
    weighted = strength[:, None] * vector_block
    keys_end = (key_block - jnp.dot(key_solve.T, weighted, precision=highest)).astype(jnp.bfloat16)
    transfer = jnp.eye(head_width, dtype=jnp.float32) - jnp.dot(
        vector_block.T, strength[:, None] * vector_solve, precision=highest
    )
    query_dots = jnp.where(causal, jnp.dot(query_block, vector_block.T, precision=highest), 0.0)
    scaled_dots = query_dots * strength[None, :]
    intra_scores = jnp.dot(query_block, key_block.T, precision=highest) - jnp.dot(
        scaled_dots, key_solve, precision=highest
    )
    rotated = query_block - jnp.dot(scaled_dots, vector_solve, precision=highest)
    return (intra_scores, keys_end, transfer, rotated)


def on_device(
    queries, key_states, value_states, transition_vectors, beta_logit, document_ids, out_weight
):
    block_rows = queries.shape[0]
    head_count = beta_logit.shape[1]
    head_width = queries.shape[1] // head_count
    score_scale = head_width ** (-0.5)

    def split_heads(flat):
        return jnp.transpose(flat.reshape(block_rows, head_count, head_width), (1, 0, 2))

    query_heads = split_heads(queries).astype(jnp.float32)
    key_heads = split_heads(key_states).astype(jnp.float32)
    value_heads = split_heads(value_states)
    vector_heads = split_heads(transition_vectors).astype(jnp.float32)
    unit_vectors = vector_heads / jnp.sqrt(
        jnp.sum(vector_heads * vector_heads, axis=2, keepdims=True) + epsilon
    )
    strength = 2.0 * jax.nn.sigmoid(beta_logit.T)
    intra_scores, keys_end, transfer, rotated = jax.vmap(shard_operators)(
        query_heads, key_heads, unit_vectors, strength
    )
    row_ids = jnp.arange(block_rows)
    causal = row_ids[:, None] >= row_ids[None, :]
    doc_float = (document_ids + 1).astype(jnp.float32)
    same_doc = doc_float[:, None] == doc_float[None, :]
    own_scores = jnp.where((causal & same_doc)[None], intra_scores * score_scale, masked_value)
    running_max = jnp.max(own_scores, axis=2)
    weights = jnp.exp(own_scores - running_max[..., None])
    running_sum = jnp.sum(weights, axis=2)
    accumulated = jnp.einsum(
        "hqk,hkd->hqd",
        weights.astype(jnp.bfloat16),
        value_heads,
        preferred_element_type=jnp.float32,
    )
    ctx_index = lax.axis_index("ctx")
    ctx_count = lax.axis_size("ctx")
    every_value = lax.all_gather(value_heads, "ctx", axis=1, tiled=True)

    def attend(carried, key_pair, value_pair, transfer_in, key_docs, is_live):
        turned, running_max, running_sum, accumulated = carried
        scores = jnp.einsum(
            "hqd,hkd->hqk",
            turned.astype(jnp.bfloat16),
            key_pair,
            preferred_element_type=jnp.float32,
        )
        allowed = (doc_float[:, None] == key_docs[None, :]) & is_live
        scores = jnp.where(allowed[None], scores * score_scale, masked_value)
        new_max = jnp.maximum(running_max, jnp.max(scores, axis=2))
        factor = jnp.exp(running_max - new_max)
        weights = jnp.exp(scores - new_max[..., None])
        running_sum = running_sum * factor + jnp.sum(weights, axis=2)
        accumulated = accumulated * factor[..., None] + jnp.einsum(
            "hqk,hkd->hqd",
            weights.astype(jnp.bfloat16),
            value_pair,
            preferred_element_type=jnp.float32,
        )
        turned = jnp.einsum("hqd,hde->hqe", turned, transfer_in, precision=highest)
        return (turned, new_max, running_sum, accumulated)

    def visit(carried, key_pair, value_pair, transfer_in, key_docs, is_live):
        return attend(carried, key_pair, value_pair, transfer_in, key_docs, is_live)

    carried = (rotated, running_max, running_sum, accumulated)
    every_key = lax.all_gather(keys_end, "ctx", axis=1, tiled=True)
    every_transfer, every_doc = (
        lax.all_gather(transfer[None].astype(jnp.bfloat16), "ctx", axis=0, tiled=True).astype(
            jnp.float32
        ),
        lax.all_gather(doc_float.astype(jnp.bfloat16), "ctx", axis=0, tiled=True).astype(
            doc_float.dtype
        ),
    )

    def local_step(offset, inner):
        source = jnp.maximum(ctx_index - offset, 0)
        key_pair = lax.dynamic_slice_in_dim(every_key, source * block_rows, block_rows, 1)
        value_pair = lax.dynamic_slice_in_dim(every_value, source * block_rows, block_rows, 1)
        transfer_in = lax.dynamic_index_in_dim(every_transfer, source, 0, keepdims=False)
        key_docs = lax.dynamic_slice_in_dim(every_doc, source * block_rows, block_rows, 0)
        return visit(inner, key_pair, value_pair, transfer_in, key_docs, ctx_index - offset >= 0)

    carried = lax.fori_loop(1, ctx_count, local_step, carried)
    attended = (carried[3] / carried[2][..., None]).astype(jnp.bfloat16)
    token_rows = jnp.transpose(attended, (1, 0, 2)).reshape(block_rows, head_count * head_width)
    return lax.psum_scatter(
        jnp.dot(token_rows, out_weight, preferred_element_type=jnp.float32).astype(jnp.bfloat16),
        "head",
        scatter_dimension=0,
        tiled=True,
    )


def solution(mesh):
    return jax.shard_map(
        on_device,
        mesh=mesh,
        in_specs=(
            P("ctx", "head"),
            P("ctx", "head"),
            P("ctx", "head"),
            P("ctx", "head"),
            P("ctx", "head"),
            P("ctx"),
            P("head", None),
        ),
        out_specs=P(("ctx", "head"), None),
        check_vma=False,
    )
```

```python
import jax
import jax.numpy as jnp
from jax import lax
from jax.sharding import PartitionSpec as P

epsilon = 1e-06
masked_value = -1e30
highest = lax.Precision.HIGHEST


def tile_inverse(tiles):
    width = tiles.shape[-1]
    row_ids = jnp.arange(width)[:, None]
    col_ids = jnp.arange(width)[None, :]
    identity = jnp.eye(width, dtype=jnp.float32)
    leaf_part = jnp.where((row_ids // 8) == (col_ids // 8), tiles, 0.0)
    square = jnp.matmul(leaf_part, leaf_part, precision=highest)
    fourth = jnp.matmul(square, square, precision=highest)
    inverse = jnp.matmul(identity - leaf_part, identity + square, precision=highest)
    inverse = jnp.matmul(inverse, identity + fourth, precision=highest)
    size = 8
    while size < width:
        pair_lower = (
            ((row_ids // (2 * size)) == (col_ids // (2 * size)))
            & ((row_ids // size) % 2 == 1)
            & ((col_ids // size) % 2 == 0)
        )
        corner = jnp.where(pair_lower, tiles, 0.0)
        inverse = inverse - jnp.matmul(
            inverse, jnp.matmul(corner, inverse, precision=highest), precision=highest
        )
        size *= 2
    return inverse


def unit_lower_inverse(strict_lower):
    rows_total = strict_lower.shape[0]
    tile = 128
    count = rows_total // tile
    blocks = [
        strict_lower[q * tile:(q + 1) * tile, q * tile:(q + 1) * tile][None] for q in range(count)
    ]
    inverses = list(tile_inverse(jnp.concatenate(blocks, axis=0)))
    size = tile
    while size < rows_total:
        merged = []
        for p in range(len(inverses) // 2):
            first = inverses[2 * p]
            second = inverses[2 * p + 1]
            start = 2 * p * size
            lower = strict_lower[start + size:start + 2 * size, start:start + size]
            corner = -jnp.dot(second, jnp.dot(lower, first, precision=highest), precision=highest)
            top = jnp.concatenate([first, jnp.zeros_like(first)], axis=1)
            bottom = jnp.concatenate([corner, second], axis=1)
            merged.append(jnp.concatenate([top, bottom], axis=0))
        inverses = merged
        size *= 2
    return inverses[0]


def lower_solve(strict_lower, right):
    rows_total = strict_lower.shape[0]
    tile = 128
    count = rows_total // tile
    if rows_total % tile or count & (count - 1):
        unit_lower = strict_lower + jnp.eye(rows_total, dtype=jnp.float32)
        return lax.linalg.triangular_solve(
            unit_lower, right, left_side=True, lower=True, unit_diagonal=True
        )
    return jnp.dot(unit_lower_inverse(strict_lower), right, precision=highest)


def shard_operators(query_block, key_block, vector_block, strength):
    block_rows = key_block.shape[0]
    head_width = key_block.shape[1]
    row_ids = jnp.arange(block_rows)
    strict = row_ids[:, None] > row_ids[None, :]
    causal = row_ids[:, None] >= row_ids[None, :]
    intersections = jnp.dot(vector_block, vector_block.T, precision=highest)
    strict_lower = jnp.where(strict, intersections * strength[None, :], 0.0)
    key_proj = jnp.where(strict, jnp.dot(vector_block, key_block.T, precision=highest), 0.0)
    solved = lower_solve(strict_lower, jnp.concatenate([key_proj, vector_block], axis=1))
    key_solve = solved[:, :block_rows]
    vector_solve = solved[:, block_rows:]
    weighted = strength[:, None] * vector_block
    keys_end = (key_block - jnp.dot(key_solve.T, weighted, precision=highest)).astype(jnp.bfloat16)
    transfer = jnp.eye(head_width, dtype=jnp.float32) - jnp.dot(
        vector_block.T, strength[:, None] * vector_solve, precision=highest
    )
    query_dots = jnp.where(causal, jnp.dot(query_block, vector_block.T, precision=highest), 0.0)
    scaled_dots = query_dots * strength[None, :]
    intra_scores = jnp.dot(query_block, key_block.T, precision=highest) - jnp.dot(
        scaled_dots, key_solve, precision=highest
    )
    rotated = query_block - jnp.dot(scaled_dots, vector_solve, precision=highest)
    return (intra_scores, keys_end, transfer, rotated)


def on_device(
    queries, key_states, value_states, transition_vectors, beta_logit, document_ids, out_weight
):
    block_rows = queries.shape[0]
    head_count = beta_logit.shape[1]
    head_width = queries.shape[1] // head_count
    score_scale = head_width ** (-0.5)

    def split_heads(flat):
        return jnp.transpose(flat.reshape(block_rows, head_count, head_width), (1, 0, 2))

    query_heads = split_heads(queries).astype(jnp.float32)
    key_heads = split_heads(key_states).astype(jnp.float32)
    value_heads = split_heads(value_states)
    vector_heads = split_heads(transition_vectors).astype(jnp.float32)
    unit_vectors = vector_heads / jnp.sqrt(
        jnp.sum(vector_heads * vector_heads, axis=2, keepdims=True) + epsilon
    )
    strength = 2.0 * jax.nn.sigmoid(beta_logit.T)
    intra_scores, keys_end, transfer, rotated = jax.vmap(shard_operators)(
        query_heads, key_heads, unit_vectors, strength
    )
    row_ids = jnp.arange(block_rows)
    causal = row_ids[:, None] >= row_ids[None, :]
    doc_float = (document_ids + 1).astype(jnp.float32)
    same_doc = doc_float[:, None] == doc_float[None, :]
    own_scores = jnp.where((causal & same_doc)[None], intra_scores * score_scale, masked_value)
    running_max = jnp.max(own_scores, axis=2)
    weights = jnp.exp(own_scores - running_max[..., None])
    running_sum = jnp.sum(weights, axis=2)
    accumulated = jnp.einsum(
        "hqk,hkd->hqd",
        weights.astype(jnp.bfloat16),
        value_heads,
        preferred_element_type=jnp.float32,
    )
    ctx_index = lax.axis_index("ctx")
    ctx_count = lax.axis_size("ctx")
    every_value = lax.all_gather(value_heads, "ctx", axis=1, tiled=True)

    def attend(carried, key_pair, value_pair, transfer_in, key_docs, is_live):
        turned, running_max, running_sum, accumulated = carried
        scores = jnp.einsum(
            "hqd,hkd->hqk",
            turned.astype(jnp.bfloat16),
            key_pair,
            preferred_element_type=jnp.float32,
        )
        allowed = (doc_float[:, None] == key_docs[None, :]) & is_live
        scores = jnp.where(allowed[None], scores * score_scale, masked_value)
        new_max = jnp.maximum(running_max, jnp.max(scores, axis=2))
        factor = jnp.exp(running_max - new_max)
        weights = jnp.exp(scores - new_max[..., None])
        running_sum = running_sum * factor + jnp.sum(weights, axis=2)
        accumulated = accumulated * factor[..., None] + jnp.einsum(
            "hqk,hkd->hqd",
            weights.astype(jnp.bfloat16),
            value_pair,
            preferred_element_type=jnp.float32,
        )
        turned = jnp.einsum("hqd,hde->hqe", turned, transfer_in, precision=highest)
        return (turned, new_max, running_sum, accumulated)

    def visit(carried, key_pair, value_pair, transfer_in, key_docs, is_live):
        return attend(carried, key_pair, value_pair, transfer_in, key_docs, is_live)

    carried = (rotated, running_max, running_sum, accumulated)
    every_key = lax.all_gather(keys_end, "ctx", axis=1, tiled=True)
    every_transfer, every_doc = (
        lax.all_gather(transfer[None].astype(jnp.bfloat16), "ctx", axis=0, tiled=True).astype(
            jnp.float32
        ),
        lax.all_gather(doc_float.astype(jnp.bfloat16), "ctx", axis=0, tiled=True).astype(
            doc_float.dtype
        ),
    )

    def local_step(offset, inner):
        source = jnp.maximum(ctx_index - offset, 0)
        key_pair = lax.dynamic_slice_in_dim(every_key, source * block_rows, block_rows, 1)
        value_pair = lax.dynamic_slice_in_dim(every_value, source * block_rows, block_rows, 1)
        transfer_in = lax.dynamic_index_in_dim(every_transfer, source, 0, keepdims=False)
        key_docs = lax.dynamic_slice_in_dim(every_doc, source * block_rows, block_rows, 0)
        return visit(inner, key_pair, value_pair, transfer_in, key_docs, ctx_index - offset >= 0)

    carried = lax.fori_loop(1, ctx_count, local_step, carried)
    attended = (carried[3] / carried[2][..., None]).astype(jnp.bfloat16)
    token_rows = jnp.transpose(attended, (1, 0, 2)).reshape(block_rows, head_count * head_width)
    return lax.psum_scatter(
        jnp.dot(token_rows, out_weight, preferred_element_type=jnp.float32).astype(jnp.bfloat16),
        "head",
        scatter_dimension=0,
        tiled=True,
    )


def solution(mesh):
    return jax.shard_map(
        on_device,
        mesh=mesh,
        in_specs=(
            P("ctx", "head"),
            P("ctx", "head"),
            P("ctx", "head"),
            P("ctx", "head"),
            P("ctx", "head"),
            P("ctx"),
            P("head", None),
        ),
        out_specs=P(("ctx", "head"), None),
        check_vma=False,
    )
```

```python
import jax
import jax.numpy as jnp
from jax import lax
from jax.sharding import PartitionSpec as P

epsilon = 1e-06
masked_value = -1e30
highest = lax.Precision.HIGHEST


def tile_inverse(tiles):
    width = tiles.shape[-1]
    row_ids = jnp.arange(width)[:, None]
    col_ids = jnp.arange(width)[None, :]
    identity = jnp.eye(width, dtype=jnp.float32)
    leaf_part = jnp.where((row_ids // 8) == (col_ids // 8), tiles, 0.0)
    square = jnp.matmul(leaf_part, leaf_part, precision=highest)
    fourth = jnp.matmul(square, square, precision=highest)
    inverse = jnp.matmul(identity - leaf_part, identity + square, precision=highest)
    inverse = jnp.matmul(inverse, identity + fourth, precision=highest)
    size = 8
    while size < width:
        pair_lower = (
            ((row_ids // (2 * size)) == (col_ids // (2 * size)))
            & ((row_ids // size) % 2 == 1)
            & ((col_ids // size) % 2 == 0)
        )
        corner = jnp.where(pair_lower, tiles, 0.0)
        inverse = inverse - jnp.matmul(
            inverse, jnp.matmul(corner, inverse, precision=highest), precision=highest
        )
        size *= 2
    return inverse


def unit_lower_inverse(strict_lower):
    rows_total = strict_lower.shape[0]
    tile = 128
    count = rows_total // tile
    blocks = [
        strict_lower[q * tile:(q + 1) * tile, q * tile:(q + 1) * tile][None] for q in range(count)
    ]
    inverses = list(tile_inverse(jnp.concatenate(blocks, axis=0)))
    size = tile
    while size < rows_total:
        merged = []
        for p in range(len(inverses) // 2):
            first = inverses[2 * p]
            second = inverses[2 * p + 1]
            start = 2 * p * size
            lower = strict_lower[start + size:start + 2 * size, start:start + size]
            corner = -jnp.dot(second, jnp.dot(lower, first, precision=highest), precision=highest)
            top = jnp.concatenate([first, jnp.zeros_like(first)], axis=1)
            bottom = jnp.concatenate([corner, second], axis=1)
            merged.append(jnp.concatenate([top, bottom], axis=0))
        inverses = merged
        size *= 2
    return inverses[0]


def lower_solve(strict_lower, right):
    rows_total = strict_lower.shape[0]
    tile = 128
    count = rows_total // tile
    if rows_total % tile or count & (count - 1):
        unit_lower = strict_lower + jnp.eye(rows_total, dtype=jnp.float32)
        return lax.linalg.triangular_solve(
            unit_lower, right, left_side=True, lower=True, unit_diagonal=True
        )
    return jnp.dot(unit_lower_inverse(strict_lower), right, precision=highest)


def shard_operators(query_block, key_block, vector_block, strength):
    block_rows = key_block.shape[0]
    head_width = key_block.shape[1]
    row_ids = jnp.arange(block_rows)
    strict = row_ids[:, None] > row_ids[None, :]
    causal = row_ids[:, None] >= row_ids[None, :]
    intersections = jnp.dot(vector_block, vector_block.T, precision=highest)
    strict_lower = jnp.where(strict, intersections * strength[None, :], 0.0)
    key_proj = jnp.where(strict, jnp.dot(vector_block, key_block.T, precision=highest), 0.0)
    solved = lower_solve(strict_lower, jnp.concatenate([key_proj, vector_block], axis=1))
    key_solve = solved[:, :block_rows]
    vector_solve = solved[:, block_rows:]
    weighted = strength[:, None] * vector_block
    keys_end = (key_block - jnp.dot(key_solve.T, weighted, precision=highest)).astype(jnp.bfloat16)
    transfer = jnp.eye(head_width, dtype=jnp.float32) - jnp.dot(
        vector_block.T, strength[:, None] * vector_solve, precision=highest
    )
    query_dots = jnp.where(causal, jnp.dot(query_block, vector_block.T, precision=highest), 0.0)
    scaled_dots = query_dots * strength[None, :]
    intra_scores = jnp.dot(query_block, key_block.T, precision=highest) - jnp.dot(
        scaled_dots, key_solve, precision=highest
    )
    rotated = query_block - jnp.dot(scaled_dots, vector_solve, precision=highest)
    return (intra_scores, keys_end, transfer, rotated)


def on_device(
    queries, key_states, value_states, transition_vectors, beta_logit, document_ids, out_weight
):
    block_rows = queries.shape[0]
    head_count = beta_logit.shape[1]
    head_width = queries.shape[1] // head_count
    score_scale = head_width ** (-0.5)

    def split_heads(flat):
        return jnp.transpose(flat.reshape(block_rows, head_count, head_width), (1, 0, 2))

    query_heads = split_heads(queries).astype(jnp.float32)
    key_heads = split_heads(key_states).astype(jnp.float32)
    value_heads = split_heads(value_states)
    vector_heads = split_heads(transition_vectors).astype(jnp.float32)
    value_columns = jnp.transpose(value_states.reshape(block_rows, head_count, head_width), (1, 2, 0))
    value_columns, vector_heads = lax.optimization_barrier((value_columns, vector_heads))
    unit_vectors = vector_heads / jnp.sqrt(
        jnp.sum(vector_heads * vector_heads, axis=2, keepdims=True) + epsilon
    )
    strength = 2.0 * jax.nn.sigmoid(beta_logit.T)
    every_value = lax.all_gather(value_columns, "ctx", axis=2, tiled=True)
    intra_scores, keys_end, transfer, rotated = jax.vmap(shard_operators)(
        query_heads, key_heads, unit_vectors, strength
    )
    every_value, keys_end = lax.optimization_barrier((every_value, keys_end))
    row_ids = jnp.arange(block_rows)
    causal = row_ids[:, None] >= row_ids[None, :]
    doc_float = (document_ids + 1).astype(jnp.float32)
    same_doc = doc_float[:, None] == doc_float[None, :]
    own_scores = jnp.where((causal & same_doc)[None], intra_scores * score_scale, masked_value)
    running_max = jnp.max(own_scores, axis=2)
    weights = jnp.exp(own_scores - running_max[..., None])
    running_sum = jnp.sum(weights, axis=2)
    accumulated = jnp.einsum(
        "hqk,hkd->hqd",
        weights.astype(jnp.bfloat16),
        value_heads,
        preferred_element_type=jnp.float32,
    )
    ctx_index = lax.axis_index("ctx")
    ctx_count = lax.axis_size("ctx")

    def attend(carried, key_pair, value_pair, transfer_in, key_docs):
        turned, running_max, running_sum, accumulated = carried
        scores = jnp.einsum(
            "hqd,hkd->hqk",
            turned.astype(jnp.bfloat16),
            key_pair,
            preferred_element_type=jnp.float32,
        )
        allowed = doc_float[:, None] == key_docs[None, :]
        scores = jnp.where(allowed[None], scores * score_scale, masked_value)
        new_max = jnp.maximum(running_max, jnp.max(scores, axis=2))
        factor = jnp.exp(running_max - new_max)
        weights = jnp.exp(scores - new_max[..., None])
        running_sum = running_sum * factor + jnp.sum(weights, axis=2)
        accumulated = accumulated * factor[..., None] + jnp.einsum(
            "hqk,hdk->hqd",
            weights.astype(jnp.bfloat16),
            value_pair,
            preferred_element_type=jnp.float32,
        )
        turned = jnp.einsum("hqd,hde->hqe", turned, transfer_in, precision=highest)
        return (turned, new_max, running_sum, accumulated)

    carried = (rotated, running_max, running_sum, accumulated)
    every_key = lax.all_gather(keys_end, "ctx", axis=1, tiled=True)
    doc_rows = doc_float.reshape(-1, head_width)
    pad_rows = (-doc_rows.shape[0]) % 8
    doc_rows = jnp.concatenate([doc_rows, jnp.zeros((pad_rows, head_width), jnp.float32)], axis=0)
    transfer_rows = jnp.concatenate(
        [transfer.reshape(head_count * head_width, head_width), doc_rows], axis=0
    ).astype(jnp.bfloat16)
    every_rows = lax.all_gather(transfer_rows[None], "ctx", axis=0, tiled=True).astype(jnp.float32)
    every_transfer = every_rows[:, : head_count * head_width].reshape(
        ctx_count, head_count, head_width, head_width
    )
    every_doc = every_rows[:, head_count * head_width :].reshape(ctx_count, -1)[:, :block_rows]
    first_doc = doc_float[0]

    def live(state):
        offset = state[0]
        source = jnp.maximum(ctx_index - offset, 0)
        last_doc = lax.dynamic_index_in_dim(every_doc, source, 0, keepdims=False)[block_rows - 1]
        return (ctx_index - offset >= 0) & (last_doc == first_doc)

    def local_step(state):
        offset, inner = state
        source = ctx_index - offset
        key_pair = lax.dynamic_slice_in_dim(every_key, source * block_rows, block_rows, 1)
        value_pair = lax.dynamic_slice_in_dim(every_value, source * block_rows, block_rows, 2)
        transfer_in = lax.dynamic_index_in_dim(every_transfer, source, 0, keepdims=False)
        key_docs = lax.dynamic_index_in_dim(every_doc, source, 0, keepdims=False)
        return (offset + 1, attend(inner, key_pair, value_pair, transfer_in, key_docs))

    carried = lax.while_loop(live, local_step, (jnp.int32(1), carried))[1]
    attended = (carried[3] / carried[2][..., None]).astype(jnp.bfloat16)
    token_rows = jnp.transpose(attended, (1, 0, 2)).reshape(block_rows, head_count * head_width)
    return lax.psum_scatter(
        jnp.dot(token_rows, out_weight, preferred_element_type=jnp.float32).astype(jnp.bfloat16),
        "head",
        scatter_dimension=0,
        tiled=True,
    )


def solution(mesh):
    return jax.shard_map(
        on_device,
        mesh=mesh,
        in_specs=(
            P("ctx", "head"),
            P("ctx", "head"),
            P("ctx", "head"),
            P("ctx", "head"),
            P("ctx", "head"),
            P("ctx"),
            P("head", None),
        ),
        out_specs=P(("ctx", "head"), None),
        check_vma=False,
    )
```

```python
import jax
import jax.numpy as jnp
from jax import lax
from jax.sharding import PartitionSpec as P

epsilon = 1e-06
masked_value = -1e30
highest = lax.Precision.HIGHEST


def tile_inverse(tiles):
    width = tiles.shape[-1]
    row_ids = jnp.arange(width)[:, None]
    col_ids = jnp.arange(width)[None, :]
    identity = jnp.eye(width, dtype=jnp.float32)
    leaf_part = jnp.where((row_ids // 8) == (col_ids // 8), tiles, 0.0)
    square = jnp.matmul(leaf_part, leaf_part, precision=highest)
    fourth = jnp.matmul(square, square, precision=highest)
    inverse = jnp.matmul(identity - leaf_part, identity + square, precision=highest)
    inverse = jnp.matmul(inverse, identity + fourth, precision=highest)
    size = 8
    while size < width:
        pair_lower = (
            ((row_ids // (2 * size)) == (col_ids // (2 * size)))
            & ((row_ids // size) % 2 == 1)
            & ((col_ids // size) % 2 == 0)
        )
        corner = jnp.where(pair_lower, tiles, 0.0)
        inverse = inverse - jnp.matmul(
            inverse, jnp.matmul(corner, inverse, precision=highest), precision=highest
        )
        size *= 2
    return inverse


def unit_lower_inverse(strict_lower):
    rows_total = strict_lower.shape[0]
    tile = 128
    count = rows_total // tile
    blocks = [
        strict_lower[q * tile:(q + 1) * tile, q * tile:(q + 1) * tile][None] for q in range(count)
    ]
    inverses = list(tile_inverse(jnp.concatenate(blocks, axis=0)))
    size = tile
    while size < rows_total:
        merged = []
        for p in range(len(inverses) // 2):
            first = inverses[2 * p]
            second = inverses[2 * p + 1]
            start = 2 * p * size
            lower = strict_lower[start + size:start + 2 * size, start:start + size]
            corner = -jnp.dot(second, jnp.dot(lower, first, precision=highest), precision=highest)
            top = jnp.concatenate([first, jnp.zeros_like(first)], axis=1)
            bottom = jnp.concatenate([corner, second], axis=1)
            merged.append(jnp.concatenate([top, bottom], axis=0))
        inverses = merged
        size *= 2
    return inverses[0]


def lower_solve(strict_lower, right):
    rows_total = strict_lower.shape[0]
    tile = 128
    count = rows_total // tile
    if rows_total % tile or count & (count - 1):
        unit_lower = strict_lower + jnp.eye(rows_total, dtype=jnp.float32)
        return lax.linalg.triangular_solve(
            unit_lower, right, left_side=True, lower=True, unit_diagonal=True
        )
    return jnp.dot(unit_lower_inverse(strict_lower), right, precision=highest)


def shard_operators(query_block, key_block, vector_block, strength):
    block_rows = key_block.shape[0]
    head_width = key_block.shape[1]
    row_ids = jnp.arange(block_rows)
    strict = row_ids[:, None] > row_ids[None, :]
    causal = row_ids[:, None] >= row_ids[None, :]
    intersections = jnp.dot(vector_block, vector_block.T, precision=highest)
    strict_lower = jnp.where(strict, intersections * strength[None, :], 0.0)
    key_proj = jnp.where(strict, jnp.dot(vector_block, key_block.T, precision=highest), 0.0)
    solved = lower_solve(strict_lower, jnp.concatenate([key_proj, vector_block], axis=1))
    key_solve = solved[:, :block_rows]
    vector_solve = solved[:, block_rows:]
    weighted = strength[:, None] * vector_block
    keys_end = (key_block - jnp.dot(key_solve.T, weighted, precision=highest)).astype(jnp.bfloat16)
    transfer = jnp.eye(head_width, dtype=jnp.float32) - jnp.dot(
        vector_block.T, strength[:, None] * vector_solve, precision=highest
    )
    query_dots = jnp.where(causal, jnp.dot(query_block, vector_block.T, precision=highest), 0.0)
    scaled_dots = query_dots * strength[None, :]
    intra_scores = jnp.dot(query_block, key_block.T, precision=highest) - jnp.dot(
        scaled_dots, key_solve, precision=highest
    )
    rotated = query_block - jnp.dot(scaled_dots, vector_solve, precision=highest)
    return (intra_scores, keys_end, transfer, rotated)


def on_device(
    queries, key_states, value_states, transition_vectors, beta_logit, document_ids, out_weight
):
    block_rows = queries.shape[0]
    head_count = beta_logit.shape[1]
    head_width = queries.shape[1] // head_count
    score_scale = head_width ** (-0.5)

    def split_heads(flat):
        return jnp.transpose(flat.reshape(block_rows, head_count, head_width), (1, 0, 2))

    query_heads = split_heads(queries).astype(jnp.float32)
    key_heads = split_heads(key_states).astype(jnp.float32)
    value_heads = split_heads(value_states)
    vector_heads = split_heads(transition_vectors).astype(jnp.float32)
    value_columns = jnp.transpose(value_states.reshape(block_rows, head_count, head_width), (1, 2, 0))
    value_columns, vector_heads = lax.optimization_barrier((value_columns, vector_heads))
    unit_vectors = vector_heads / jnp.sqrt(
        jnp.sum(vector_heads * vector_heads, axis=2, keepdims=True) + epsilon
    )
    strength = 2.0 * jax.nn.sigmoid(beta_logit.T)
    every_value = lax.all_gather(value_columns, "ctx", axis=2, tiled=True)
    intra_scores, keys_end, transfer, rotated = jax.vmap(shard_operators)(
        query_heads, key_heads, unit_vectors, strength
    )
    every_value, keys_end = lax.optimization_barrier((every_value, keys_end))
    row_ids = jnp.arange(block_rows)
    causal = row_ids[:, None] >= row_ids[None, :]
    doc_float = (document_ids + 1).astype(jnp.float32)
    same_doc = doc_float[:, None] == doc_float[None, :]
    own_scores = jnp.where((causal & same_doc)[None], intra_scores * score_scale, masked_value)
    running_max = jnp.max(own_scores, axis=2)
    weights = jnp.exp(own_scores - running_max[..., None])
    running_sum = jnp.sum(weights, axis=2)
    accumulated = jnp.einsum(
        "hqk,hkd->hqd",
        weights.astype(jnp.bfloat16),
        value_heads,
        preferred_element_type=jnp.float32,
    )
    ctx_index = lax.axis_index("ctx")
    ctx_count = lax.axis_size("ctx")

    def attend(carried, key_pair, value_pair, transfer_in, key_docs):
        turned, running_max, running_sum, accumulated = carried
        scores = jnp.einsum(
            "hqd,hkd->hqk",
            turned.astype(jnp.bfloat16),
            key_pair,
            preferred_element_type=jnp.float32,
        )
        allowed = doc_float[:, None] == key_docs[None, :]
        scores = jnp.where(allowed[None], scores * score_scale, masked_value)
        new_max = jnp.maximum(running_max, jnp.max(scores, axis=2))
        factor = jnp.exp(running_max - new_max)
        weights = jnp.exp(scores - new_max[..., None])
        running_sum = running_sum * factor + jnp.sum(weights, axis=2)
        accumulated = accumulated * factor[..., None] + jnp.einsum(
            "hqk,hdk->hqd",
            weights.astype(jnp.bfloat16),
            value_pair,
            preferred_element_type=jnp.float32,
        )
        turned = jnp.einsum("hqd,hde->hqe", turned, transfer_in, precision=highest)
        return (turned, new_max, running_sum, accumulated)

    carried = (rotated, running_max, running_sum, accumulated)
    doc_rows = doc_float.reshape(-1, head_width)
    pad_rows = (-doc_rows.shape[0]) % 8
    doc_rows = jnp.concatenate([doc_rows, jnp.zeros((pad_rows, head_width), jnp.float32)], axis=0)
    doc_rows = jnp.broadcast_to(doc_rows.astype(jnp.bfloat16)[None], (head_count,) + doc_rows.shape)
    key_rows = jnp.concatenate([keys_end, transfer.astype(jnp.bfloat16), doc_rows], axis=1)
    stride = key_rows.shape[1]
    every_rows = lax.all_gather(key_rows, "ctx", axis=1, tiled=True)
    every_doc = (
        every_rows[0].reshape(ctx_count, stride, head_width)[:, block_rows + head_width :]
        .reshape(ctx_count, -1)[:, :block_rows]
        .astype(jnp.float32)
    )
    first_doc = doc_float[0]

    def live(state):
        offset = state[0]
        source = jnp.maximum(ctx_index - offset, 0)
        last_doc = lax.dynamic_index_in_dim(every_doc, source, 0, keepdims=False)[block_rows - 1]
        return (ctx_index - offset >= 0) & (last_doc == first_doc)

    def local_step(state):
        offset, inner = state
        source = ctx_index - offset
        key_pair = lax.dynamic_slice_in_dim(every_rows, source * stride, block_rows, 1)
        value_pair = lax.dynamic_slice_in_dim(every_value, source * block_rows, block_rows, 2)
        transfer_in = lax.dynamic_slice_in_dim(
            every_rows, source * stride + block_rows, head_width, 1
        ).astype(jnp.float32)
        key_docs = lax.dynamic_index_in_dim(every_doc, source, 0, keepdims=False)
        return (offset + 1, attend(inner, key_pair, value_pair, transfer_in, key_docs))

    carried = lax.while_loop(live, local_step, (jnp.int32(1), carried))[1]
    attended = (carried[3] / carried[2][..., None]).astype(jnp.bfloat16)
    token_rows = jnp.transpose(attended, (1, 0, 2)).reshape(block_rows, head_count * head_width)
    return lax.psum_scatter(
        jnp.dot(token_rows, out_weight, preferred_element_type=jnp.float32).astype(jnp.bfloat16),
        "head",
        scatter_dimension=0,
        tiled=True,
    )


def solution(mesh):
    return jax.shard_map(
        on_device,
        mesh=mesh,
        in_specs=(
            P("ctx", "head"),
            P("ctx", "head"),
            P("ctx", "head"),
            P("ctx", "head"),
            P("ctx", "head"),
            P("ctx"),
            P("head", None),
        ),
        out_specs=P(("ctx", "head"), None),
        check_vma=False,
    )
```

```python
import jax
import jax.numpy as jnp
from jax import lax
from jax.sharding import PartitionSpec as P

epsilon = 1e-06
masked_value = -1e30
highest = lax.Precision.HIGHEST


def tile_inverse(tiles):
    width = tiles.shape[-1]
    row_ids = jnp.arange(width)[:, None]
    col_ids = jnp.arange(width)[None, :]
    identity = jnp.eye(width, dtype=jnp.float32)
    leaf_part = jnp.where((row_ids // 8) == (col_ids // 8), tiles, 0.0)
    square = jnp.matmul(leaf_part, leaf_part, precision=highest)
    fourth = jnp.matmul(square, square, precision=highest)
    inverse = jnp.matmul(identity - leaf_part, identity + square, precision=highest)
    inverse = jnp.matmul(inverse, identity + fourth, precision=highest)
    size = 8
    while size < width:
        pair_lower = (
            ((row_ids // (2 * size)) == (col_ids // (2 * size)))
            & ((row_ids // size) % 2 == 1)
            & ((col_ids // size) % 2 == 0)
        )
        corner = jnp.where(pair_lower, tiles, 0.0)
        inverse = inverse - jnp.matmul(
            inverse, jnp.matmul(corner, inverse, precision=highest), precision=highest
        )
        size *= 2
    return inverse


def unit_lower_inverse(strict_lower):
    rows_total = strict_lower.shape[0]
    tile = 128
    count = rows_total // tile
    blocks = [
        strict_lower[q * tile:(q + 1) * tile, q * tile:(q + 1) * tile][None] for q in range(count)
    ]
    inverses = list(tile_inverse(jnp.concatenate(blocks, axis=0)))
    size = tile
    while size < rows_total:
        merged = []
        for p in range(len(inverses) // 2):
            first = inverses[2 * p]
            second = inverses[2 * p + 1]
            start = 2 * p * size
            lower = strict_lower[start + size:start + 2 * size, start:start + size]
            corner = -jnp.dot(second, jnp.dot(lower, first, precision=highest), precision=highest)
            top = jnp.concatenate([first, jnp.zeros_like(first)], axis=1)
            bottom = jnp.concatenate([corner, second], axis=1)
            merged.append(jnp.concatenate([top, bottom], axis=0))
        inverses = merged
        size *= 2
    return inverses[0]


def lower_solve(strict_lower, right):
    rows_total = strict_lower.shape[0]
    tile = 128
    count = rows_total // tile
    if rows_total % tile or count & (count - 1):
        unit_lower = strict_lower + jnp.eye(rows_total, dtype=jnp.float32)
        return lax.linalg.triangular_solve(
            unit_lower, right, left_side=True, lower=True, unit_diagonal=True
        )
    return jnp.dot(unit_lower_inverse(strict_lower), right, precision=highest)


def shard_operators(query_block, key_block, vector_block, strength):
    block_rows = key_block.shape[0]
    head_width = key_block.shape[1]
    row_ids = jnp.arange(block_rows)
    strict = row_ids[:, None] > row_ids[None, :]
    causal = row_ids[:, None] >= row_ids[None, :]
    intersections = jnp.dot(vector_block, vector_block.T, precision=highest)
    strict_lower = jnp.where(strict, intersections * strength[None, :], 0.0)
    key_proj = jnp.where(strict, jnp.dot(vector_block, key_block.T, precision=highest), 0.0)
    solved = lower_solve(strict_lower, jnp.concatenate([key_proj, vector_block], axis=1))
    key_solve = solved[:, :block_rows]
    vector_solve = solved[:, block_rows:]
    weighted = strength[:, None] * vector_block
    keys_end = (key_block - jnp.dot(key_solve.T, weighted, precision=highest)).astype(jnp.bfloat16)
    transfer = jnp.eye(head_width, dtype=jnp.float32) - jnp.dot(
        vector_block.T, strength[:, None] * vector_solve, precision=highest
    )
    query_dots = jnp.where(causal, jnp.dot(query_block, vector_block.T, precision=highest), 0.0)
    scaled_dots = query_dots * strength[None, :]
    intra_scores = jnp.dot(query_block, key_block.T, precision=highest) - jnp.dot(
        scaled_dots, key_solve, precision=highest
    )
    rotated = query_block - jnp.dot(scaled_dots, vector_solve, precision=highest)
    return (intra_scores, keys_end, transfer, rotated)


def on_device(
    queries, key_states, value_states, transition_vectors, beta_logit, document_ids, out_weight
):
    block_rows = queries.shape[0]
    head_count = beta_logit.shape[1]
    head_width = queries.shape[1] // head_count
    score_scale = head_width ** (-0.5)

    def split_heads(flat):
        return jnp.transpose(flat.reshape(block_rows, head_count, head_width), (1, 0, 2))

    query_heads = split_heads(queries).astype(jnp.float32)
    key_heads = split_heads(key_states).astype(jnp.float32)
    value_heads = split_heads(value_states)
    vector_heads = split_heads(transition_vectors).astype(jnp.float32)
    value_columns = jnp.transpose(value_states.reshape(block_rows, head_count, head_width), (1, 2, 0))
    value_columns, vector_heads = lax.optimization_barrier((value_columns, vector_heads))
    unit_vectors = vector_heads / jnp.sqrt(
        jnp.sum(vector_heads * vector_heads, axis=2, keepdims=True) + epsilon
    )
    strength = 2.0 * jax.nn.sigmoid(beta_logit.T)
    every_value = lax.all_gather(value_columns, "ctx", axis=2, tiled=True)
    intra_scores, keys_end, transfer, rotated = jax.vmap(shard_operators)(
        query_heads, key_heads, unit_vectors, strength
    )
    every_value, keys_end = lax.optimization_barrier((every_value, keys_end))
    row_ids = jnp.arange(block_rows)
    causal = row_ids[:, None] >= row_ids[None, :]
    doc_float = (document_ids + 1).astype(jnp.float32)
    same_doc = doc_float[:, None] == doc_float[None, :]
    own_scores = jnp.where((causal & same_doc)[None], intra_scores * score_scale, masked_value)
    running_max = jnp.max(own_scores, axis=2)
    weights = jnp.exp(own_scores - running_max[..., None])
    running_sum = jnp.sum(weights, axis=2)
    accumulated = jnp.einsum(
        "hqk,hkd->hqd",
        weights.astype(jnp.bfloat16),
        value_heads,
        preferred_element_type=jnp.float32,
    )
    ctx_index = lax.axis_index("ctx")
    ctx_count = lax.axis_size("ctx")

    def attend(carried, key_pair, value_pair, transfer_in, key_docs):
        turned, running_max, running_sum, accumulated = carried
        scores = jnp.einsum(
            "hqd,hkd->hqk",
            turned.astype(jnp.bfloat16),
            key_pair,
            preferred_element_type=jnp.float32,
        )
        allowed = doc_float[:, None] == key_docs[None, :]
        scores = jnp.where(allowed[None], scores * score_scale, masked_value)
        new_max = jnp.maximum(running_max, jnp.max(scores, axis=2))
        factor = jnp.exp(running_max - new_max)
        weights = jnp.exp(scores - new_max[..., None])
        running_sum = running_sum * factor + jnp.sum(weights, axis=2)
        accumulated = accumulated * factor[..., None] + jnp.einsum(
            "hqk,hdk->hqd",
            weights.astype(jnp.bfloat16),
            value_pair,
            preferred_element_type=jnp.float32,
        )
        turned = jnp.einsum("hqd,hde->hqe", turned, transfer_in, precision=highest)
        return (turned, new_max, running_sum, accumulated)

    carried = (rotated, running_max, running_sum, accumulated)
    doc_rows = doc_float.reshape(-1, head_width)
    pad_rows = (-doc_rows.shape[0]) % 8
    doc_rows = jnp.concatenate([doc_rows, jnp.zeros((pad_rows, head_width), jnp.float32)], axis=0)
    meta_rows = jnp.concatenate(
        [transfer.reshape(head_count * head_width, head_width), doc_rows], axis=0
    ).astype(jnp.bfloat16)
    first_doc = doc_float[0]
    is_live = jnp.bool_(True)
    for offset in range(1, ctx_count):
        pairs = [(s, s + offset) for s in range(ctx_count - offset)]
        key_pair = lax.ppermute(keys_end, "ctx", pairs)
        meta_in = lax.ppermute(meta_rows, "ctx", pairs).astype(jnp.float32)
        transfer_in = meta_in[: head_count * head_width].reshape(head_count, head_width, head_width)
        key_docs = meta_in[head_count * head_width :].reshape(-1)[:block_rows]
        source = jnp.maximum(ctx_index - offset, 0)
        value_pair = lax.dynamic_slice_in_dim(every_value, source * block_rows, block_rows, 2)
        is_live = is_live & (ctx_index - offset >= 0) & (key_docs[block_rows - 1] == first_doc)
        carried = lax.cond(
            is_live,
            lambda inner, k=key_pair, v=value_pair, t=transfer_in, d=key_docs: attend(inner, k, v, t, d),
            lambda inner: inner,
            carried,
        )
    attended = (carried[3] / carried[2][..., None]).astype(jnp.bfloat16)
    token_rows = jnp.transpose(attended, (1, 0, 2)).reshape(block_rows, head_count * head_width)
    return lax.psum_scatter(
        jnp.dot(token_rows, out_weight, preferred_element_type=jnp.float32).astype(jnp.bfloat16),
        "head",
        scatter_dimension=0,
        tiled=True,
    )


def solution(mesh):
    return jax.shard_map(
        on_device,
        mesh=mesh,
        in_specs=(
            P("ctx", "head"),
            P("ctx", "head"),
            P("ctx", "head"),
            P("ctx", "head"),
            P("ctx", "head"),
            P("ctx"),
            P("head", None),
        ),
        out_specs=P(("ctx", "head"), None),
        check_vma=False,
    )
```

```python
import jax
import jax.numpy as jnp
from jax import lax
from jax.sharding import PartitionSpec as P

epsilon = 1e-06
masked_value = -1e30
highest = lax.Precision.HIGHEST


def tile_inverse(tiles):
    width = tiles.shape[-1]
    row_ids = jnp.arange(width)[:, None]
    col_ids = jnp.arange(width)[None, :]
    identity = jnp.eye(width, dtype=jnp.float32)
    leaf_part = jnp.where((row_ids // 8) == (col_ids // 8), tiles, 0.0)
    square = jnp.matmul(leaf_part, leaf_part, precision=highest)
    fourth = jnp.matmul(square, square, precision=highest)
    inverse = jnp.matmul(identity - leaf_part, identity + square, precision=highest)
    inverse = jnp.matmul(inverse, identity + fourth, precision=highest)
    size = 8
    while size < width:
        pair_lower = (
            ((row_ids // (2 * size)) == (col_ids // (2 * size)))
            & ((row_ids // size) % 2 == 1)
            & ((col_ids // size) % 2 == 0)
        )
        corner = jnp.where(pair_lower, tiles, 0.0)
        inverse = inverse - jnp.matmul(
            inverse, jnp.matmul(corner, inverse, precision=highest), precision=highest
        )
        size *= 2
    return inverse


def unit_lower_inverse(strict_lower):
    rows_total = strict_lower.shape[0]
    tile = 128
    count = rows_total // tile
    blocks = [
        strict_lower[q * tile:(q + 1) * tile, q * tile:(q + 1) * tile][None] for q in range(count)
    ]
    inverses = list(tile_inverse(jnp.concatenate(blocks, axis=0)))
    size = tile
    while size < rows_total:
        merged = []
        for p in range(len(inverses) // 2):
            first = inverses[2 * p]
            second = inverses[2 * p + 1]
            start = 2 * p * size
            lower = strict_lower[start + size:start + 2 * size, start:start + size]
            corner = -jnp.dot(second, jnp.dot(lower, first, precision=highest), precision=highest)
            top = jnp.concatenate([first, jnp.zeros_like(first)], axis=1)
            bottom = jnp.concatenate([corner, second], axis=1)
            merged.append(jnp.concatenate([top, bottom], axis=0))
        inverses = merged
        size *= 2
    return inverses[0]


def lower_solve(strict_lower, right):
    rows_total = strict_lower.shape[0]
    tile = 128
    count = rows_total // tile
    if rows_total % tile or count & (count - 1):
        unit_lower = strict_lower + jnp.eye(rows_total, dtype=jnp.float32)
        return lax.linalg.triangular_solve(
            unit_lower, right, left_side=True, lower=True, unit_diagonal=True
        )
    return jnp.dot(unit_lower_inverse(strict_lower), right, precision=highest)


def shard_operators(query_block, key_block, vector_block, strength):
    block_rows = key_block.shape[0]
    head_width = key_block.shape[1]
    row_ids = jnp.arange(block_rows)
    strict = row_ids[:, None] > row_ids[None, :]
    causal = row_ids[:, None] >= row_ids[None, :]
    intersections = jnp.dot(vector_block, vector_block.T, precision=highest)
    strict_lower = jnp.where(strict, intersections * strength[None, :], 0.0)
    key_proj = jnp.where(strict, jnp.dot(vector_block, key_block.T, precision=highest), 0.0)
    solved = lower_solve(strict_lower, jnp.concatenate([key_proj, vector_block], axis=1))
    key_solve = solved[:, :block_rows]
    vector_solve = solved[:, block_rows:]
    weighted = strength[:, None] * vector_block
    keys_end = (key_block - jnp.dot(key_solve.T, weighted, precision=highest)).astype(jnp.bfloat16)
    transfer = jnp.eye(head_width, dtype=jnp.float32) - jnp.dot(
        vector_block.T, strength[:, None] * vector_solve, precision=highest
    )
    query_dots = jnp.where(causal, jnp.dot(query_block, vector_block.T, precision=highest), 0.0)
    scaled_dots = query_dots * strength[None, :]
    intra_scores = jnp.dot(query_block, key_block.T, precision=highest) - jnp.dot(
        scaled_dots, key_solve, precision=highest
    )
    rotated = query_block - jnp.dot(scaled_dots, vector_solve, precision=highest)
    return (intra_scores, keys_end, transfer, rotated)


def on_device(
    queries, key_states, value_states, transition_vectors, beta_logit, document_ids, out_weight
):
    block_rows = queries.shape[0]
    head_count = beta_logit.shape[1]
    head_width = queries.shape[1] // head_count
    score_scale = head_width ** (-0.5)

    def split_heads(flat):
        return jnp.transpose(flat.reshape(block_rows, head_count, head_width), (1, 0, 2))

    query_heads = split_heads(queries).astype(jnp.float32)
    key_heads = split_heads(key_states).astype(jnp.float32)
    value_heads = split_heads(value_states)
    vector_heads = split_heads(transition_vectors).astype(jnp.float32)
    value_columns = jnp.transpose(value_states.reshape(block_rows, head_count, head_width), (1, 2, 0))
    value_columns, vector_heads = lax.optimization_barrier((value_columns, vector_heads))
    unit_vectors = vector_heads / jnp.sqrt(
        jnp.sum(vector_heads * vector_heads, axis=2, keepdims=True) + epsilon
    )
    strength = 2.0 * jax.nn.sigmoid(beta_logit.T)
    every_value = lax.all_gather(value_columns, "ctx", axis=2, tiled=True)
    intra_scores, keys_end, transfer, rotated = jax.vmap(shard_operators)(
        query_heads, key_heads, unit_vectors, strength
    )
    every_value, keys_end = lax.optimization_barrier((every_value, keys_end))
    row_ids = jnp.arange(block_rows)
    causal = row_ids[:, None] >= row_ids[None, :]
    doc_float = (document_ids + 1).astype(jnp.float32)
    same_doc = doc_float[:, None] == doc_float[None, :]
    own_scores = jnp.where((causal & same_doc)[None], intra_scores * score_scale, masked_value)
    running_max = jnp.max(own_scores, axis=2)
    weights = jnp.exp(own_scores - running_max[..., None])
    running_sum = jnp.sum(weights, axis=2)
    accumulated = jnp.einsum(
        "hqk,hkd->hqd",
        weights.astype(jnp.bfloat16),
        value_heads,
        preferred_element_type=jnp.float32,
    )
    ctx_index = lax.axis_index("ctx")
    ctx_count = lax.axis_size("ctx")

    def attend(carried, key_pair, value_pair, transfer_in, key_docs):
        turned, running_max, running_sum, accumulated = carried
        scores = jnp.einsum(
            "hqd,hkd->hqk",
            turned.astype(jnp.bfloat16),
            key_pair,
            preferred_element_type=jnp.float32,
        )
        allowed = doc_float[:, None] == key_docs[None, :]
        scores = jnp.where(allowed[None], scores * score_scale, masked_value)
        new_max = jnp.maximum(running_max, jnp.max(scores, axis=2))
        factor = jnp.exp(running_max - new_max)
        weights = jnp.exp(scores - new_max[..., None])
        running_sum = running_sum * factor + jnp.sum(weights, axis=2)
        accumulated = accumulated * factor[..., None] + jnp.einsum(
            "hqk,hdk->hqd",
            weights.astype(jnp.bfloat16),
            value_pair,
            preferred_element_type=jnp.float32,
        )
        turned = jnp.einsum("hqd,hde->hqe", turned, transfer_in, precision=highest)
        return (turned, new_max, running_sum, accumulated)

    carried = (rotated, running_max, running_sum, accumulated)
    doc_rows = doc_float.reshape(-1, head_width)
    pad_rows = (-doc_rows.shape[0]) % 8
    doc_rows = jnp.concatenate([doc_rows, jnp.zeros((pad_rows, head_width), jnp.float32)], axis=0)
    meta_rows = jnp.concatenate(
        [transfer.reshape(head_count * head_width, head_width), doc_rows], axis=0
    ).astype(jnp.bfloat16)
    first_doc = doc_float[0]
    every_key = lax.all_gather(keys_end, "ctx", axis=1, tiled=True)
    is_live = jnp.bool_(True)
    for offset in range(1, ctx_count):
        pairs = [(s, s + offset) for s in range(ctx_count - offset)]
        meta_in = lax.ppermute(meta_rows, "ctx", pairs).astype(jnp.float32)
        transfer_in = meta_in[: head_count * head_width].reshape(head_count, head_width, head_width)
        key_docs = meta_in[head_count * head_width :].reshape(-1)[:block_rows]
        source = jnp.maximum(ctx_index - offset, 0)
        value_pair = lax.dynamic_slice_in_dim(every_value, source * block_rows, block_rows, 2)
        key_pair = lax.dynamic_slice_in_dim(every_key, source * block_rows, block_rows, 1)
        is_live = is_live & (ctx_index - offset >= 0) & (key_docs[block_rows - 1] == first_doc)
        carried = lax.cond(
            is_live,
            lambda inner, k=key_pair, v=value_pair, t=transfer_in, d=key_docs: attend(inner, k, v, t, d),
            lambda inner: inner,
            carried,
        )
    attended = (carried[3] / carried[2][..., None]).astype(jnp.bfloat16)
    token_rows = jnp.transpose(attended, (1, 0, 2)).reshape(block_rows, head_count * head_width)
    return lax.psum_scatter(
        jnp.dot(token_rows, out_weight, preferred_element_type=jnp.float32).astype(jnp.bfloat16),
        "head",
        scatter_dimension=0,
        tiled=True,
    )


def solution(mesh):
    return jax.shard_map(
        on_device,
        mesh=mesh,
        in_specs=(
            P("ctx", "head"),
            P("ctx", "head"),
            P("ctx", "head"),
            P("ctx", "head"),
            P("ctx", "head"),
            P("ctx"),
            P("head", None),
        ),
        out_specs=P(("ctx", "head"), None),
        check_vma=False,
    )
```

```python
import jax
import jax.numpy as jnp
from jax import lax
from jax.sharding import PartitionSpec as P

epsilon = 1e-06
masked_value = -1e30
highest = lax.Precision.HIGHEST


def tile_inverse(tiles):
    width = tiles.shape[-1]
    row_ids = jnp.arange(width)[:, None]
    col_ids = jnp.arange(width)[None, :]
    identity = jnp.eye(width, dtype=jnp.float32)
    leaf_part = jnp.where((row_ids // 8) == (col_ids // 8), tiles, 0.0)
    square = jnp.matmul(leaf_part, leaf_part, precision=highest)
    fourth = jnp.matmul(square, square, precision=highest)
    inverse = jnp.matmul(identity - leaf_part, identity + square, precision=highest)
    inverse = jnp.matmul(inverse, identity + fourth, precision=highest)
    size = 8
    while size < width:
        pair_lower = (
            ((row_ids // (2 * size)) == (col_ids // (2 * size)))
            & ((row_ids // size) % 2 == 1)
            & ((col_ids // size) % 2 == 0)
        )
        corner = jnp.where(pair_lower, tiles, 0.0)
        inverse = inverse - jnp.matmul(
            inverse, jnp.matmul(corner, inverse, precision=highest), precision=highest
        )
        size *= 2
    return inverse


def unit_lower_inverse(strict_lower):
    rows_total = strict_lower.shape[0]
    tile = 128
    count = rows_total // tile
    blocks = [
        strict_lower[q * tile:(q + 1) * tile, q * tile:(q + 1) * tile][None] for q in range(count)
    ]
    inverses = list(tile_inverse(jnp.concatenate(blocks, axis=0)))
    size = tile
    while size < rows_total:
        merged = []
        for p in range(len(inverses) // 2):
            first = inverses[2 * p]
            second = inverses[2 * p + 1]
            start = 2 * p * size
            lower = strict_lower[start + size:start + 2 * size, start:start + size]
            corner = -jnp.dot(second, jnp.dot(lower, first, precision=highest), precision=highest)
            top = jnp.concatenate([first, jnp.zeros_like(first)], axis=1)
            bottom = jnp.concatenate([corner, second], axis=1)
            merged.append(jnp.concatenate([top, bottom], axis=0))
        inverses = merged
        size *= 2
    return inverses[0]


def lower_solve(strict_lower, right):
    rows_total = strict_lower.shape[0]
    tile = 128
    count = rows_total // tile
    if rows_total % tile or count & (count - 1):
        unit_lower = strict_lower + jnp.eye(rows_total, dtype=jnp.float32)
        return lax.linalg.triangular_solve(
            unit_lower, right, left_side=True, lower=True, unit_diagonal=True
        )
    return jnp.dot(unit_lower_inverse(strict_lower), right, precision=highest)


def shard_operators(query_block, key_block, vector_block, strength):
    block_rows = key_block.shape[0]
    head_width = key_block.shape[1]
    row_ids = jnp.arange(block_rows)
    strict = row_ids[:, None] > row_ids[None, :]
    causal = row_ids[:, None] >= row_ids[None, :]
    intersections = jnp.dot(vector_block, vector_block.T, precision=highest)
    strict_lower = jnp.where(strict, intersections * strength[None, :], 0.0)
    key_proj = jnp.where(strict, jnp.dot(vector_block, key_block.T, precision=highest), 0.0)
    solved = lower_solve(strict_lower, jnp.concatenate([key_proj, vector_block], axis=1))
    key_solve = solved[:, :block_rows]
    vector_solve = solved[:, block_rows:]
    weighted = strength[:, None] * vector_block
    keys_end = (key_block - jnp.dot(key_solve.T, weighted, precision=highest)).astype(jnp.bfloat16)
    transfer = jnp.eye(head_width, dtype=jnp.float32) - jnp.dot(
        vector_block.T, strength[:, None] * vector_solve, precision=highest
    )
    query_dots = jnp.where(causal, jnp.dot(query_block, vector_block.T, precision=highest), 0.0)
    scaled_dots = query_dots * strength[None, :]
    intra_scores = jnp.dot(query_block, key_block.T, precision=highest) - jnp.dot(
        scaled_dots, key_solve, precision=highest
    )
    rotated = query_block - jnp.dot(scaled_dots, vector_solve, precision=highest)
    return (intra_scores, keys_end, transfer, rotated)


def on_device(
    queries, key_states, value_states, transition_vectors, beta_logit, document_ids, out_weight
):
    block_rows = queries.shape[0]
    head_count = beta_logit.shape[1]
    head_width = queries.shape[1] // head_count
    score_scale = head_width ** (-0.5)

    def split_heads(flat):
        return jnp.transpose(flat.reshape(block_rows, head_count, head_width), (1, 0, 2))

    query_heads = split_heads(queries).astype(jnp.float32)
    key_heads = split_heads(key_states).astype(jnp.float32)
    value_heads = split_heads(value_states)
    vector_heads = split_heads(transition_vectors).astype(jnp.float32)
    value_columns = jnp.transpose(value_states.reshape(block_rows, head_count, head_width), (1, 2, 0))
    value_columns, vector_heads = lax.optimization_barrier((value_columns, vector_heads))
    unit_vectors = vector_heads / jnp.sqrt(
        jnp.sum(vector_heads * vector_heads, axis=2, keepdims=True) + epsilon
    )
    strength = 2.0 * jax.nn.sigmoid(beta_logit.T)
    every_value = lax.all_gather(value_columns, "ctx", axis=2, tiled=True)
    intra_scores, keys_end, transfer, rotated = jax.vmap(shard_operators)(
        query_heads, key_heads, unit_vectors, strength
    )
    every_value, keys_end = lax.optimization_barrier((every_value, keys_end))
    row_ids = jnp.arange(block_rows)
    causal = row_ids[:, None] >= row_ids[None, :]
    doc_float = (document_ids + 1).astype(jnp.float32)
    same_doc = doc_float[:, None] == doc_float[None, :]
    own_scores = jnp.where((causal & same_doc)[None], intra_scores * score_scale, masked_value)
    running_max = jnp.max(own_scores, axis=2)
    weights = jnp.exp(own_scores - running_max[..., None])
    running_sum = jnp.sum(weights, axis=2)
    accumulated = jnp.einsum(
        "hqk,hkd->hqd",
        weights.astype(jnp.bfloat16),
        value_heads,
        preferred_element_type=jnp.float32,
    )
    ctx_index = lax.axis_index("ctx")
    ctx_count = lax.axis_size("ctx")

    def attend(carried, key_pair, value_pair, transfer_in, key_docs):
        turned, running_max, running_sum, accumulated = carried
        scores = jnp.einsum(
            "hqd,hkd->hqk",
            turned.astype(jnp.bfloat16),
            key_pair,
            preferred_element_type=jnp.float32,
        )
        allowed = doc_float[:, None] == key_docs[None, :]
        scores = jnp.where(allowed[None], scores * score_scale, masked_value)
        new_max = jnp.maximum(running_max, jnp.max(scores, axis=2))
        factor = jnp.exp(running_max - new_max)
        weights = jnp.exp(scores - new_max[..., None])
        running_sum = running_sum * factor + jnp.sum(weights, axis=2)
        accumulated = accumulated * factor[..., None] + jnp.einsum(
            "hqk,hdk->hqd",
            weights.astype(jnp.bfloat16),
            value_pair,
            preferred_element_type=jnp.float32,
        )
        turned = jnp.einsum("hqd,hde->hqe", turned, transfer_in, precision=highest)
        return (turned, new_max, running_sum, accumulated)

    carried = (rotated, running_max, running_sum, accumulated)
    doc_rows = doc_float.reshape(-1, head_width)
    pad_rows = (-doc_rows.shape[0]) % 8
    doc_rows = jnp.concatenate([doc_rows, jnp.zeros((pad_rows, head_width), jnp.float32)], axis=0)
    meta_rows = jnp.concatenate(
        [transfer.reshape(head_count * head_width, head_width), doc_rows], axis=0
    ).astype(jnp.bfloat16)
    first_doc = doc_float[0]
    every_key = lax.all_gather(keys_end, "ctx", axis=1, tiled=True)
    is_live = jnp.bool_(True)
    steps = []
    for offset in range(1, ctx_count):
        pairs = [(s, s + offset) for s in range(ctx_count - offset)]
        meta_in = lax.ppermute(meta_rows, "ctx", pairs).astype(jnp.float32)
        transfer_in = meta_in[: head_count * head_width].reshape(head_count, head_width, head_width)
        key_docs = meta_in[head_count * head_width :].reshape(-1)[:block_rows]
        is_live = is_live & (ctx_index - offset >= 0) & (key_docs[block_rows - 1] == first_doc)
        steps.append((offset, transfer_in, key_docs, is_live))

    def chain(index, inner):
        if index == len(steps):
            return inner
        offset, transfer_in, key_docs, step_live = steps[index]

        def take(inner):
            source = jnp.maximum(ctx_index - offset, 0)
            value_pair = lax.dynamic_slice_in_dim(every_value, source * block_rows, block_rows, 2)
            key_pair = lax.dynamic_slice_in_dim(every_key, source * block_rows, block_rows, 1)
            return chain(index + 1, attend(inner, key_pair, value_pair, transfer_in, key_docs))

        return lax.cond(step_live, take, lambda inner: inner, inner)

    carried = chain(0, carried)
    attended = (carried[3] / carried[2][..., None]).astype(jnp.bfloat16)
    token_rows = jnp.transpose(attended, (1, 0, 2)).reshape(block_rows, head_count * head_width)
    projected = jnp.dot(token_rows, out_weight, preferred_element_type=jnp.float32)
    return scatter_sum(projected).astype(jnp.bfloat16)


def scatter_sum(projected):
    head_count = lax.axis_size("head")
    if head_count % 2:
        return lax.psum_scatter(projected, "head", scatter_dimension=0, tiled=True)
    chips = head_count // 2
    rows = projected.shape[0] // head_count
    head_index = lax.axis_index("head")
    core = head_index % 2
    chip = head_index // 2
    grouped = projected.reshape(chips, 2, rows, projected.shape[1])
    mine = lax.dynamic_index_in_dim(grouped, core, 1, keepdims=False)
    other = lax.dynamic_index_in_dim(grouped, 1 - core, 1, keepdims=False)
    partner = [(h, h ^ 1) for h in range(head_count)]
    chip_sum = mine + lax.ppermute(other.astype(jnp.bfloat16), "head", partner).astype(jnp.float32)
    total = lax.dynamic_index_in_dim(chip_sum, chip, 0, keepdims=False)
    for shift in range(1, chips):
        pairs = [
            (2 * y + c, 2 * ((y + shift) % chips) + c) for y in range(chips) for c in range(2)
        ]
        outgoing = lax.dynamic_index_in_dim(chip_sum, (chip + shift) % chips, 0, keepdims=False)
        total = total + lax.ppermute(outgoing.astype(jnp.bfloat16), "head", pairs).astype(jnp.float32)
    return total


def solution(mesh):
    return jax.shard_map(
        on_device,
        mesh=mesh,
        in_specs=(
            P("ctx", "head"),
            P("ctx", "head"),
            P("ctx", "head"),
            P("ctx", "head"),
            P("ctx", "head"),
            P("ctx"),
            P("head", None),
        ),
        out_specs=P(("ctx", "head"), None),
        check_vma=False,
    )
```

```python
import jax
import jax.numpy as jnp
from jax import lax
from jax.sharding import PartitionSpec as P

epsilon = 1e-06
masked_value = -1e30
highest = lax.Precision.HIGHEST


def tile_inverse(tiles):
    width = tiles.shape[-1]
    row_ids = jnp.arange(width)[:, None]
    col_ids = jnp.arange(width)[None, :]
    identity = jnp.eye(width, dtype=jnp.float32)
    leaf_part = jnp.where((row_ids // 8) == (col_ids // 8), tiles, 0.0)
    square = jnp.matmul(leaf_part, leaf_part, precision=highest)
    fourth = jnp.matmul(square, square, precision=highest)
    inverse = jnp.matmul(identity - leaf_part, identity + square, precision=highest)
    inverse = jnp.matmul(inverse, identity + fourth, precision=highest)
    size = 8
    while size < width:
        pair_lower = (
            ((row_ids // (2 * size)) == (col_ids // (2 * size)))
            & ((row_ids // size) % 2 == 1)
            & ((col_ids // size) % 2 == 0)
        )
        corner = jnp.where(pair_lower, tiles, 0.0)
        inverse = inverse - jnp.matmul(
            inverse, jnp.matmul(corner, inverse, precision=highest), precision=highest
        )
        size *= 2
    return inverse


def unit_lower_inverse(strict_lower):
    rows_total = strict_lower.shape[0]
    tile = 128
    count = rows_total // tile
    blocks = [
        strict_lower[q * tile:(q + 1) * tile, q * tile:(q + 1) * tile][None] for q in range(count)
    ]
    inverses = list(tile_inverse(jnp.concatenate(blocks, axis=0)))
    size = tile
    while size < rows_total:
        merged = []
        for p in range(len(inverses) // 2):
            first = inverses[2 * p]
            second = inverses[2 * p + 1]
            start = 2 * p * size
            lower = strict_lower[start + size:start + 2 * size, start:start + size]
            corner = -jnp.dot(second, jnp.dot(lower, first, precision=highest), precision=highest)
            top = jnp.concatenate([first, jnp.zeros_like(first)], axis=1)
            bottom = jnp.concatenate([corner, second], axis=1)
            merged.append(jnp.concatenate([top, bottom], axis=0))
        inverses = merged
        size *= 2
    return inverses[0]


def lower_solve(strict_lower, right):
    rows_total = strict_lower.shape[0]
    tile = 128
    count = rows_total // tile
    if rows_total % tile or count & (count - 1):
        unit_lower = strict_lower + jnp.eye(rows_total, dtype=jnp.float32)
        return lax.linalg.triangular_solve(
            unit_lower, right, left_side=True, lower=True, unit_diagonal=True
        )
    return jnp.dot(unit_lower_inverse(strict_lower), right, precision=highest)


def shard_operators(query_block, key_block, vector_block, strength):
    block_rows = key_block.shape[0]
    head_width = key_block.shape[1]
    row_ids = jnp.arange(block_rows)
    strict = row_ids[:, None] > row_ids[None, :]
    causal = row_ids[:, None] >= row_ids[None, :]
    intersections = jnp.dot(vector_block, vector_block.T, precision=highest)
    strict_lower = jnp.where(strict, intersections * strength[None, :], 0.0)
    key_proj = jnp.where(strict, jnp.dot(vector_block, key_block.T, precision=highest), 0.0)
    solved = lower_solve(strict_lower, jnp.concatenate([key_proj, vector_block], axis=1))
    key_solve = solved[:, :block_rows]
    vector_solve = solved[:, block_rows:]
    weighted = strength[:, None] * vector_block
    keys_end = (key_block - jnp.dot(key_solve.T, weighted, precision=highest)).astype(jnp.bfloat16)
    transfer = jnp.eye(head_width, dtype=jnp.float32) - jnp.dot(
        vector_block.T, strength[:, None] * vector_solve, precision=highest
    )
    query_dots = jnp.where(causal, jnp.dot(query_block, vector_block.T, precision=highest), 0.0)
    scaled_dots = query_dots * strength[None, :]
    intra_scores = jnp.dot(query_block, key_block.T, precision=highest) - jnp.dot(
        scaled_dots, key_solve, precision=highest
    )
    rotated = query_block - jnp.dot(scaled_dots, vector_solve, precision=highest)
    return (intra_scores, keys_end, transfer, rotated)


def on_device(
    queries, key_states, value_states, transition_vectors, beta_logit, document_ids, out_weight
):
    block_rows = queries.shape[0]
    head_count = beta_logit.shape[1]
    head_width = queries.shape[1] // head_count
    score_scale = head_width ** (-0.5)

    def split_heads(flat):
        return jnp.transpose(flat.reshape(block_rows, head_count, head_width), (1, 0, 2))

    query_heads = split_heads(queries).astype(jnp.float32)
    key_heads = split_heads(key_states).astype(jnp.float32)
    value_heads = split_heads(value_states)
    vector_heads = split_heads(transition_vectors).astype(jnp.float32)
    value_columns = jnp.transpose(value_states.reshape(block_rows, head_count, head_width), (1, 2, 0))
    value_columns, vector_heads = lax.optimization_barrier((value_columns, vector_heads))
    unit_vectors = vector_heads / jnp.sqrt(
        jnp.sum(vector_heads * vector_heads, axis=2, keepdims=True) + epsilon
    )
    strength = 2.0 * jax.nn.sigmoid(beta_logit.T)
    every_value = lax.all_gather(value_columns, "ctx", axis=2, tiled=True)
    intra_scores, keys_end, transfer, rotated = jax.vmap(shard_operators)(
        query_heads, key_heads, unit_vectors, strength
    )
    every_value, keys_end = lax.optimization_barrier((every_value, keys_end))
    row_ids = jnp.arange(block_rows)
    causal = row_ids[:, None] >= row_ids[None, :]
    doc_float = (document_ids + 1).astype(jnp.float32)
    same_doc = doc_float[:, None] == doc_float[None, :]
    own_scores = jnp.where((causal & same_doc)[None], intra_scores * score_scale, masked_value)
    running_max = jnp.max(own_scores, axis=2)
    weights = jnp.exp(own_scores - running_max[..., None])
    running_sum = jnp.sum(weights, axis=2)
    accumulated = jnp.einsum(
        "hqk,hkd->hqd",
        weights.astype(jnp.bfloat16),
        value_heads,
        preferred_element_type=jnp.float32,
    )
    ctx_index = lax.axis_index("ctx")
    ctx_count = lax.axis_size("ctx")

    def attend(carried, key_pair, value_pair, transfer_in, key_docs):
        turned, running_max, running_sum, accumulated = carried
        scores = jnp.einsum(
            "hqd,hkd->hqk",
            turned.astype(jnp.bfloat16),
            key_pair,
            preferred_element_type=jnp.float32,
        )
        allowed = doc_float[:, None] == key_docs[None, :]
        scores = jnp.where(allowed[None], scores * score_scale, masked_value)
        new_max = jnp.maximum(running_max, jnp.max(scores, axis=2))
        factor = jnp.exp(running_max - new_max)
        weights = jnp.exp(scores - new_max[..., None])
        running_sum = running_sum * factor + jnp.sum(weights, axis=2)
        accumulated = accumulated * factor[..., None] + jnp.einsum(
            "hqk,hdk->hqd",
            weights.astype(jnp.bfloat16),
            value_pair,
            preferred_element_type=jnp.float32,
        )
        turned = jnp.einsum("hqd,hde->hqe", turned, transfer_in, precision=highest)
        return (turned, new_max, running_sum, accumulated)

    carried = (rotated, running_max, running_sum, accumulated)
    doc_rows = doc_float.reshape(-1, head_width)
    pad_rows = (-doc_rows.shape[0]) % 8
    doc_rows = jnp.concatenate([doc_rows, jnp.zeros((pad_rows, head_width), jnp.float32)], axis=0)
    meta_rows = jnp.concatenate(
        [transfer.reshape(head_count * head_width, head_width), doc_rows], axis=0
    ).astype(jnp.bfloat16)
    first_doc = doc_float[0]
    every_key = lax.all_gather(keys_end, "ctx", axis=1, tiled=True)
    is_live = jnp.bool_(True)
    steps = []
    for offset in range(1, ctx_count):
        pairs = [(s, s + offset) for s in range(ctx_count - offset)]
        meta_in = lax.ppermute(meta_rows, "ctx", pairs).astype(jnp.float32)
        transfer_in = meta_in[: head_count * head_width].reshape(head_count, head_width, head_width)
        key_docs = meta_in[head_count * head_width :].reshape(-1)[:block_rows]
        is_live = is_live & (ctx_index - offset >= 0) & (key_docs[block_rows - 1] == first_doc)
        steps.append((offset, transfer_in, key_docs, is_live))

    for offset, transfer_in, key_docs, step_live in steps:

        def take(inner, offset=offset, transfer_in=transfer_in, key_docs=key_docs):
            source = jnp.maximum(ctx_index - offset, 0)
            value_pair = lax.dynamic_slice_in_dim(every_value, source * block_rows, block_rows, 2)
            key_pair = lax.dynamic_slice_in_dim(every_key, source * block_rows, block_rows, 1)
            return attend(inner, key_pair, value_pair, transfer_in, key_docs)

        carried = lax.cond(step_live, take, lambda inner: inner, carried)
    attended = (carried[3] / carried[2][..., None]).astype(jnp.bfloat16)
    token_rows = jnp.transpose(attended, (1, 0, 2)).reshape(block_rows, head_count * head_width)
    projected = jnp.dot(token_rows, out_weight, preferred_element_type=jnp.float32)
    return scatter_sum(projected).astype(jnp.bfloat16)


def scatter_sum(projected):
    head_count = lax.axis_size("head")
    if head_count % 2:
        return lax.psum_scatter(projected, "head", scatter_dimension=0, tiled=True)
    chips = head_count // 2
    rows = projected.shape[0] // head_count
    head_index = lax.axis_index("head")
    core = head_index % 2
    chip = head_index // 2
    grouped = projected.reshape(chips, 2, rows, projected.shape[1])
    mine = lax.dynamic_index_in_dim(grouped, core, 1, keepdims=False)
    other = lax.dynamic_index_in_dim(grouped, 1 - core, 1, keepdims=False)
    partner = [(h, h ^ 1) for h in range(head_count)]
    chip_sum = mine + lax.ppermute(other.astype(jnp.bfloat16), "head", partner).astype(jnp.float32)
    total = lax.dynamic_index_in_dim(chip_sum, chip, 0, keepdims=False)
    for shift in range(1, chips):
        pairs = [
            (2 * y + c, 2 * ((y + shift) % chips) + c) for y in range(chips) for c in range(2)
        ]
        outgoing = lax.dynamic_index_in_dim(chip_sum, (chip + shift) % chips, 0, keepdims=False)
        total = total + lax.ppermute(outgoing.astype(jnp.bfloat16), "head", pairs).astype(jnp.float32)
    return total


def solution(mesh):
    return jax.shard_map(
        on_device,
        mesh=mesh,
        in_specs=(
            P("ctx", "head"),
            P("ctx", "head"),
            P("ctx", "head"),
            P("ctx", "head"),
            P("ctx", "head"),
            P("ctx"),
            P("head", None),
        ),
        out_specs=P(("ctx", "head"), None),
        check_vma=False,
    )
```

```python
import jax
import jax.numpy as jnp
from jax import lax
from jax.sharding import PartitionSpec as P

epsilon = 1e-06
masked_value = -1e30
highest = lax.Precision.HIGHEST


def tile_inverse(tiles):
    width = tiles.shape[-1]
    row_ids = jnp.arange(width)[:, None]
    col_ids = jnp.arange(width)[None, :]
    identity = jnp.eye(width, dtype=jnp.float32)
    leaf_part = jnp.where((row_ids // 8) == (col_ids // 8), tiles, 0.0)
    square = jnp.matmul(leaf_part, leaf_part, precision=highest)
    fourth = jnp.matmul(square, square, precision=highest)
    inverse = jnp.matmul(identity - leaf_part, identity + square, precision=highest)
    inverse = jnp.matmul(inverse, identity + fourth, precision=highest)
    size = 8
    while size < width:
        pair_lower = (
            ((row_ids // (2 * size)) == (col_ids // (2 * size)))
            & ((row_ids // size) % 2 == 1)
            & ((col_ids // size) % 2 == 0)
        )
        corner = jnp.where(pair_lower, tiles, 0.0)
        inverse = inverse - jnp.matmul(
            inverse, jnp.matmul(corner, inverse, precision=highest), precision=highest
        )
        size *= 2
    return inverse


def unit_lower_inverse(strict_lower):
    rows_total = strict_lower.shape[0]
    tile = 128
    count = rows_total // tile
    blocks = [
        strict_lower[q * tile:(q + 1) * tile, q * tile:(q + 1) * tile][None] for q in range(count)
    ]
    inverses = list(tile_inverse(jnp.concatenate(blocks, axis=0)))
    size = tile
    while size < rows_total:
        merged = []
        for p in range(len(inverses) // 2):
            first = inverses[2 * p]
            second = inverses[2 * p + 1]
            start = 2 * p * size
            lower = strict_lower[start + size:start + 2 * size, start:start + size]
            corner = -jnp.dot(second, jnp.dot(lower, first, precision=highest), precision=highest)
            top = jnp.concatenate([first, jnp.zeros_like(first)], axis=1)
            bottom = jnp.concatenate([corner, second], axis=1)
            merged.append(jnp.concatenate([top, bottom], axis=0))
        inverses = merged
        size *= 2
    return inverses[0]


def lower_solve(strict_lower, right):
    rows_total = strict_lower.shape[0]
    tile = 128
    count = rows_total // tile
    if rows_total % tile or count & (count - 1):
        unit_lower = strict_lower + jnp.eye(rows_total, dtype=jnp.float32)
        return lax.linalg.triangular_solve(
            unit_lower, right, left_side=True, lower=True, unit_diagonal=True
        )
    return jnp.dot(unit_lower_inverse(strict_lower), right, precision=highest)


def shard_operators(query_block, key_block, vector_block, strength):
    block_rows = key_block.shape[0]
    head_width = key_block.shape[1]
    row_ids = jnp.arange(block_rows)
    strict = row_ids[:, None] > row_ids[None, :]
    causal = row_ids[:, None] >= row_ids[None, :]
    intersections = jnp.dot(vector_block, vector_block.T, precision=highest)
    strict_lower = jnp.where(strict, intersections * strength[None, :], 0.0)
    key_proj = jnp.where(strict, jnp.dot(vector_block, key_block.T, precision=highest), 0.0)
    solved = lower_solve(strict_lower, jnp.concatenate([key_proj, vector_block], axis=1))
    key_solve = solved[:, :block_rows]
    vector_solve = solved[:, block_rows:]
    weighted = strength[:, None] * vector_block
    keys_end = (key_block - jnp.dot(key_solve.T, weighted, precision=highest)).astype(jnp.bfloat16)
    transfer = jnp.eye(head_width, dtype=jnp.float32) - jnp.dot(
        vector_block.T, strength[:, None] * vector_solve, precision=highest
    )
    query_dots = jnp.where(causal, jnp.dot(query_block, vector_block.T, precision=highest), 0.0)
    scaled_dots = query_dots * strength[None, :]
    intra_scores = jnp.dot(query_block, key_block.T, precision=highest) - jnp.dot(
        scaled_dots, key_solve, precision=highest
    )
    rotated = query_block - jnp.dot(scaled_dots, vector_solve, precision=highest)
    return (intra_scores, keys_end, transfer, rotated)


def on_device(
    queries, key_states, value_states, transition_vectors, beta_logit, document_ids, out_weight
):
    block_rows = queries.shape[0]
    head_count = beta_logit.shape[1]
    head_width = queries.shape[1] // head_count
    score_scale = head_width ** (-0.5)

    def split_heads(flat):
        return jnp.transpose(flat.reshape(block_rows, head_count, head_width), (1, 0, 2))

    query_heads = split_heads(queries).astype(jnp.float32)
    key_heads = split_heads(key_states).astype(jnp.float32)
    value_heads = split_heads(value_states)
    vector_heads = split_heads(transition_vectors).astype(jnp.float32)
    value_columns = jnp.transpose(value_states.reshape(block_rows, head_count, head_width), (1, 2, 0))
    value_columns, vector_heads = lax.optimization_barrier((value_columns, vector_heads))
    unit_vectors = vector_heads / jnp.sqrt(
        jnp.sum(vector_heads * vector_heads, axis=2, keepdims=True) + epsilon
    )
    strength = 2.0 * jax.nn.sigmoid(beta_logit.T)
    ctx_total = lax.axis_size("ctx")
    every_value = lax.all_to_all(
        jnp.broadcast_to(value_columns[None], (ctx_total,) + value_columns.shape), "ctx", 0, 0
    )
    intra_scores, keys_end, transfer, rotated = jax.vmap(shard_operators)(
        query_heads, key_heads, unit_vectors, strength
    )
    every_value, rotated = lax.optimization_barrier((every_value, rotated))
    row_ids = jnp.arange(block_rows)
    causal = row_ids[:, None] >= row_ids[None, :]
    doc_float = (document_ids + 1).astype(jnp.float32)
    same_doc = doc_float[:, None] == doc_float[None, :]
    own_scores = jnp.where((causal & same_doc)[None], intra_scores * score_scale, masked_value)
    running_max = jnp.max(own_scores, axis=2)
    weights = jnp.exp(own_scores - running_max[..., None])
    running_sum = jnp.sum(weights, axis=2)
    accumulated = jnp.einsum(
        "hqk,hkd->hqd",
        weights.astype(jnp.bfloat16),
        value_heads,
        preferred_element_type=jnp.float32,
    )
    ctx_index = lax.axis_index("ctx")
    ctx_count = lax.axis_size("ctx")

    def attend(carried, key_pair, value_pair, transfer_in, key_docs):
        turned, running_max, running_sum, accumulated = carried
        scores = jnp.einsum(
            "hqd,hkd->hqk",
            turned.astype(jnp.bfloat16),
            key_pair,
            preferred_element_type=jnp.float32,
        )
        allowed = doc_float[:, None] == key_docs[None, :]
        scores = jnp.where(allowed[None], scores * score_scale, masked_value)
        new_max = jnp.maximum(running_max, jnp.max(scores, axis=2))
        factor = jnp.exp(running_max - new_max)
        weights = jnp.exp(scores - new_max[..., None])
        running_sum = running_sum * factor + jnp.sum(weights, axis=2)
        accumulated = accumulated * factor[..., None] + jnp.einsum(
            "hqk,hdk->hqd",
            weights.astype(jnp.bfloat16),
            value_pair,
            preferred_element_type=jnp.float32,
        )
        turned = jnp.einsum("hqd,hde->hqe", turned, transfer_in, precision=highest)
        return (turned, new_max, running_sum, accumulated)

    carried = (rotated, running_max, running_sum, accumulated)
    doc_rows = doc_float.reshape(-1, head_width)
    pad_rows = (-doc_rows.shape[0]) % 8
    doc_rows = jnp.concatenate([doc_rows, jnp.zeros((pad_rows, head_width), jnp.float32)], axis=0)
    meta_rows = jnp.concatenate(
        [transfer.reshape(head_count * head_width, head_width), doc_rows], axis=0
    ).astype(jnp.bfloat16)
    first_doc = doc_float[0]
    every_key = lax.all_gather(keys_end, "ctx", axis=1, tiled=True)
    is_live = jnp.bool_(True)
    steps = []
    for offset in range(1, ctx_count):
        pairs = [(s, s + offset) for s in range(ctx_count - offset)]
        meta_in = lax.ppermute(meta_rows, "ctx", pairs).astype(jnp.float32)
        transfer_in = meta_in[: head_count * head_width].reshape(head_count, head_width, head_width)
        key_docs = meta_in[head_count * head_width :].reshape(-1)[:block_rows]
        is_live = is_live & (ctx_index - offset >= 0) & (key_docs[block_rows - 1] == first_doc)
        steps.append((offset, transfer_in, key_docs, is_live))

    for offset, transfer_in, key_docs, step_live in steps:

        def take(inner, offset=offset, transfer_in=transfer_in, key_docs=key_docs):
            source = jnp.maximum(ctx_index - offset, 0)
            value_pair = lax.dynamic_index_in_dim(every_value, source, 0, keepdims=False)
            key_pair = lax.dynamic_slice_in_dim(every_key, source * block_rows, block_rows, 1)
            return attend(inner, key_pair, value_pair, transfer_in, key_docs)

        carried = lax.cond(step_live, take, lambda inner: inner, carried)
    attended = (carried[3] / carried[2][..., None]).astype(jnp.bfloat16)
    token_rows = jnp.transpose(attended, (1, 0, 2)).reshape(block_rows, head_count * head_width)
    projected = jnp.dot(token_rows, out_weight, preferred_element_type=jnp.float32)
    return scatter_sum(projected).astype(jnp.bfloat16)


def scatter_sum(projected):
    head_count = lax.axis_size("head")
    if head_count % 2:
        return lax.psum_scatter(projected, "head", scatter_dimension=0, tiled=True)
    chips = head_count // 2
    rows = projected.shape[0] // head_count
    head_index = lax.axis_index("head")
    core = head_index % 2
    chip = head_index // 2
    grouped = projected.reshape(chips, 2, rows, projected.shape[1])
    mine = lax.dynamic_index_in_dim(grouped, core, 1, keepdims=False)
    other = lax.dynamic_index_in_dim(grouped, 1 - core, 1, keepdims=False)
    partner = [(h, h ^ 1) for h in range(head_count)]
    chip_sum = mine + lax.ppermute(other.astype(jnp.bfloat16), "head", partner).astype(jnp.float32)
    total = lax.dynamic_index_in_dim(chip_sum, chip, 0, keepdims=False)
    for shift in range(1, chips):
        pairs = [
            (2 * y + c, 2 * ((y + shift) % chips) + c) for y in range(chips) for c in range(2)
        ]
        outgoing = lax.dynamic_index_in_dim(chip_sum, (chip + shift) % chips, 0, keepdims=False)
        total = total + lax.ppermute(outgoing.astype(jnp.bfloat16), "head", pairs).astype(jnp.float32)
    return total


def solution(mesh):
    return jax.shard_map(
        on_device,
        mesh=mesh,
        in_specs=(
            P("ctx", "head"),
            P("ctx", "head"),
            P("ctx", "head"),
            P("ctx", "head"),
            P("ctx", "head"),
            P("ctx"),
            P("head", None),
        ),
        out_specs=P(("ctx", "head"), None),
        check_vma=False,
    )
```

```python
import jax
import jax.numpy as jnp
from jax import lax
from jax.sharding import PartitionSpec as P

epsilon = 1e-06
masked_value = -1e30
highest = lax.Precision.HIGHEST


def tile_inverse(tiles):
    width = tiles.shape[-1]
    row_ids = jnp.arange(width)[:, None]
    col_ids = jnp.arange(width)[None, :]
    identity = jnp.eye(width, dtype=jnp.float32)
    leaf_part = jnp.where((row_ids // 8) == (col_ids // 8), tiles, 0.0)
    square = jnp.matmul(leaf_part, leaf_part, precision=highest)
    fourth = jnp.matmul(square, square, precision=highest)
    inverse = jnp.matmul(identity - leaf_part, identity + square, precision=highest)
    inverse = jnp.matmul(inverse, identity + fourth, precision=highest)
    size = 8
    while size < width:
        pair_lower = (
            ((row_ids // (2 * size)) == (col_ids // (2 * size)))
            & ((row_ids // size) % 2 == 1)
            & ((col_ids // size) % 2 == 0)
        )
        corner = jnp.where(pair_lower, tiles, 0.0)
        inverse = inverse - jnp.matmul(
            inverse, jnp.matmul(corner, inverse, precision=highest), precision=highest
        )
        size *= 2
    return inverse


def unit_lower_inverse(strict_lower):
    rows_total = strict_lower.shape[0]
    tile = 128
    count = rows_total // tile
    blocks = [
        strict_lower[q * tile:(q + 1) * tile, q * tile:(q + 1) * tile][None] for q in range(count)
    ]
    inverses = list(tile_inverse(jnp.concatenate(blocks, axis=0)))
    size = tile
    while size < rows_total:
        merged = []
        for p in range(len(inverses) // 2):
            first = inverses[2 * p]
            second = inverses[2 * p + 1]
            start = 2 * p * size
            lower = strict_lower[start + size:start + 2 * size, start:start + size]
            corner = -jnp.dot(second, jnp.dot(lower, first, precision=highest), precision=highest)
            top = jnp.concatenate([first, jnp.zeros_like(first)], axis=1)
            bottom = jnp.concatenate([corner, second], axis=1)
            merged.append(jnp.concatenate([top, bottom], axis=0))
        inverses = merged
        size *= 2
    return inverses[0]


def lower_solve(strict_lower, right):
    rows_total = strict_lower.shape[0]
    tile = 128
    count = rows_total // tile
    if rows_total % tile or count & (count - 1):
        unit_lower = strict_lower + jnp.eye(rows_total, dtype=jnp.float32)
        return lax.linalg.triangular_solve(
            unit_lower, right, left_side=True, lower=True, unit_diagonal=True
        )
    return jnp.dot(unit_lower_inverse(strict_lower), right, precision=highest)


def shard_operators(query_block, key_block, vector_block, strength):
    block_rows = key_block.shape[0]
    head_width = key_block.shape[1]
    row_ids = jnp.arange(block_rows)
    strict = row_ids[:, None] > row_ids[None, :]
    causal = row_ids[:, None] >= row_ids[None, :]
    intersections = jnp.dot(vector_block, vector_block.T, precision=highest)
    strict_lower = jnp.where(strict, intersections * strength[None, :], 0.0)
    key_proj = jnp.where(strict, jnp.dot(vector_block, key_block.T, precision=highest), 0.0)
    solved = lower_solve(strict_lower, jnp.concatenate([key_proj, vector_block], axis=1))
    key_solve = solved[:, :block_rows]
    vector_solve = solved[:, block_rows:]
    weighted = strength[:, None] * vector_block
    keys_end = (key_block - jnp.dot(key_solve.T, weighted, precision=highest)).astype(jnp.bfloat16)
    transfer = jnp.eye(head_width, dtype=jnp.float32) - jnp.dot(
        vector_block.T, strength[:, None] * vector_solve, precision=highest
    )
    query_dots = jnp.where(causal, jnp.dot(query_block, vector_block.T, precision=highest), 0.0)
    scaled_dots = query_dots * strength[None, :]
    intra_scores = jnp.dot(query_block, key_block.T, precision=highest) - jnp.dot(
        scaled_dots, key_solve, precision=highest
    )
    rotated = query_block - jnp.dot(scaled_dots, vector_solve, precision=highest)
    return (intra_scores, keys_end, transfer, rotated)


def on_device(
    queries, key_states, value_states, transition_vectors, beta_logit, document_ids, out_weight
):
    block_rows = queries.shape[0]
    head_count = beta_logit.shape[1]
    head_width = queries.shape[1] // head_count
    score_scale = head_width ** (-0.5)

    def split_heads(flat):
        return jnp.transpose(flat.reshape(block_rows, head_count, head_width), (1, 0, 2))

    query_heads = split_heads(queries).astype(jnp.float32)
    key_heads = split_heads(key_states).astype(jnp.float32)
    value_heads = split_heads(value_states)
    vector_heads = split_heads(transition_vectors).astype(jnp.float32)
    value_columns = jnp.transpose(value_states.reshape(block_rows, head_count, head_width), (1, 2, 0))
    value_columns, vector_heads = lax.optimization_barrier((value_columns, vector_heads))
    unit_vectors = vector_heads / jnp.sqrt(
        jnp.sum(vector_heads * vector_heads, axis=2, keepdims=True) + epsilon
    )
    strength = 2.0 * jax.nn.sigmoid(beta_logit.T)
    every_value = lax.all_gather(value_columns, "ctx", axis=2, tiled=True)
    intra_scores, keys_end, transfer, rotated = jax.vmap(shard_operators)(
        query_heads, key_heads, unit_vectors, strength
    )
    every_value, keys_end = lax.optimization_barrier((every_value, keys_end))
    row_ids = jnp.arange(block_rows)
    causal = row_ids[:, None] >= row_ids[None, :]
    doc_float = (document_ids + 1).astype(jnp.float32)
    same_doc = doc_float[:, None] == doc_float[None, :]
    own_scores = jnp.where((causal & same_doc)[None], intra_scores * score_scale, masked_value)
    running_max = jnp.max(own_scores, axis=2)
    weights = jnp.exp(own_scores - running_max[..., None])
    running_sum = jnp.sum(weights, axis=2)
    accumulated = jnp.einsum(
        "hqk,hkd->hqd",
        weights.astype(jnp.bfloat16),
        value_heads,
        preferred_element_type=jnp.float32,
    )
    ctx_index = lax.axis_index("ctx")
    ctx_count = lax.axis_size("ctx")

    def attend(carried, key_pair, value_pair, transfer_in, key_docs):
        turned, running_max, running_sum, accumulated = carried
        scores = jnp.einsum(
            "hqd,hkd->hqk",
            turned.astype(jnp.bfloat16),
            key_pair,
            preferred_element_type=jnp.float32,
        )
        allowed = doc_float[:, None] == key_docs[None, :]
        scores = jnp.where(allowed[None], scores * score_scale, masked_value)
        new_max = jnp.maximum(running_max, jnp.max(scores, axis=2))
        factor = jnp.exp(running_max - new_max)
        weights = jnp.exp(scores - new_max[..., None])
        running_sum = running_sum * factor + jnp.sum(weights, axis=2)
        accumulated = accumulated * factor[..., None] + jnp.einsum(
            "hqk,hdk->hqd",
            weights.astype(jnp.bfloat16),
            value_pair,
            preferred_element_type=jnp.float32,
        )
        turned = jnp.einsum("hqd,hde->hqe", turned, transfer_in, precision=highest)
        return (turned, new_max, running_sum, accumulated)

    carried = (rotated, running_max, running_sum, accumulated)
    doc_rows = doc_float.reshape(-1, head_width)
    pad_rows = (-doc_rows.shape[0]) % 8
    doc_rows = jnp.concatenate([doc_rows, jnp.zeros((pad_rows, head_width), jnp.float32)], axis=0)
    meta_rows = jnp.concatenate(
        [transfer.reshape(head_count * head_width, head_width), doc_rows], axis=0
    ).astype(jnp.bfloat16)
    first_doc = doc_float[0]
    half = head_count // 2 if head_count % 2 == 0 else head_count
    head_groups = [(0, half), (half, head_count)] if half < head_count else [(0, head_count)]
    every_keys = [
        lax.all_gather(keys_end[lo:hi], "ctx", axis=1, tiled=True) for lo, hi in head_groups
    ]
    is_live = jnp.bool_(True)
    steps = []
    for offset in range(1, ctx_count):
        pairs = [(s, s + offset) for s in range(ctx_count - offset)]
        meta_in = lax.ppermute(meta_rows, "ctx", pairs).astype(jnp.float32)
        transfer_in = meta_in[: head_count * head_width].reshape(head_count, head_width, head_width)
        key_docs = meta_in[head_count * head_width :].reshape(-1)[:block_rows]
        is_live = is_live & (ctx_index - offset >= 0) & (key_docs[block_rows - 1] == first_doc)
        steps.append((offset, transfer_in, key_docs, is_live))

    results = []
    for (lo, hi), every_key in zip(head_groups, every_keys):
        group = tuple(part[lo:hi] for part in carried)
        for offset, transfer_in, key_docs, step_live in steps:

            def take(inner, offset=offset, transfer_in=transfer_in, key_docs=key_docs, lo=lo, hi=hi, every_key=every_key):
                source = jnp.maximum(ctx_index - offset, 0)
                value_pair = lax.dynamic_slice_in_dim(every_value[lo:hi], source * block_rows, block_rows, 2)
                key_pair = lax.dynamic_slice_in_dim(every_key, source * block_rows, block_rows, 1)
                return attend(inner, key_pair, value_pair, transfer_in[lo:hi], key_docs)

            group = lax.cond(step_live, take, lambda inner: inner, group)
        results.append(group)
    carried = tuple(jnp.concatenate(parts, axis=0) for parts in zip(*results))
    attended = (carried[3] / carried[2][..., None]).astype(jnp.bfloat16)
    token_rows = jnp.transpose(attended, (1, 0, 2)).reshape(block_rows, head_count * head_width)
    projected = jnp.dot(token_rows, out_weight, preferred_element_type=jnp.float32)
    return scatter_sum(projected).astype(jnp.bfloat16)


def scatter_sum(projected):
    head_count = lax.axis_size("head")
    if head_count % 2:
        return lax.psum_scatter(projected, "head", scatter_dimension=0, tiled=True)
    chips = head_count // 2
    rows = projected.shape[0] // head_count
    head_index = lax.axis_index("head")
    core = head_index % 2
    chip = head_index // 2
    grouped = projected.reshape(chips, 2, rows, projected.shape[1])
    mine = lax.dynamic_index_in_dim(grouped, core, 1, keepdims=False)
    other = lax.dynamic_index_in_dim(grouped, 1 - core, 1, keepdims=False)
    partner = [(h, h ^ 1) for h in range(head_count)]
    chip_sum = mine + lax.ppermute(other.astype(jnp.bfloat16), "head", partner).astype(jnp.float32)
    total = lax.dynamic_index_in_dim(chip_sum, chip, 0, keepdims=False)
    for shift in range(1, chips):
        pairs = [
            (2 * y + c, 2 * ((y + shift) % chips) + c) for y in range(chips) for c in range(2)
        ]
        outgoing = lax.dynamic_index_in_dim(chip_sum, (chip + shift) % chips, 0, keepdims=False)
        total = total + lax.ppermute(outgoing.astype(jnp.bfloat16), "head", pairs).astype(jnp.float32)
    return total


def solution(mesh):
    return jax.shard_map(
        on_device,
        mesh=mesh,
        in_specs=(
            P("ctx", "head"),
            P("ctx", "head"),
            P("ctx", "head"),
            P("ctx", "head"),
            P("ctx", "head"),
            P("ctx"),
            P("head", None),
        ),
        out_specs=P(("ctx", "head"), None),
        check_vma=False,
    )
```

```python
import jax
import jax.numpy as jnp
from jax import lax
from jax.sharding import PartitionSpec as P

epsilon = 1e-06
masked_value = -1e30
highest = lax.Precision.HIGHEST


def tile_inverse(tiles):
    width = tiles.shape[-1]
    row_ids = jnp.arange(width)[:, None]
    col_ids = jnp.arange(width)[None, :]
    identity = jnp.eye(width, dtype=jnp.float32)
    leaf_part = jnp.where((row_ids // 8) == (col_ids // 8), tiles, 0.0)
    square = jnp.matmul(leaf_part, leaf_part, precision=highest)
    fourth = jnp.matmul(square, square, precision=highest)
    inverse = jnp.matmul(identity - leaf_part, identity + square, precision=highest)
    inverse = jnp.matmul(inverse, identity + fourth, precision=highest)
    size = 8
    while size < width:
        pair_lower = (
            ((row_ids // (2 * size)) == (col_ids // (2 * size)))
            & ((row_ids // size) % 2 == 1)
            & ((col_ids // size) % 2 == 0)
        )
        corner = jnp.where(pair_lower, tiles, 0.0)
        inverse = inverse - jnp.matmul(
            inverse, jnp.matmul(corner, inverse, precision=highest), precision=highest
        )
        size *= 2
    return inverse


def unit_lower_inverse(strict_lower):
    rows_total = strict_lower.shape[0]
    tile = 128
    count = rows_total // tile
    blocks = [
        strict_lower[q * tile:(q + 1) * tile, q * tile:(q + 1) * tile][None] for q in range(count)
    ]
    inverses = list(tile_inverse(jnp.concatenate(blocks, axis=0)))
    size = tile
    while size < rows_total:
        merged = []
        for p in range(len(inverses) // 2):
            first = inverses[2 * p]
            second = inverses[2 * p + 1]
            start = 2 * p * size
            lower = strict_lower[start + size:start + 2 * size, start:start + size]
            corner = -jnp.dot(second, jnp.dot(lower, first, precision=highest), precision=highest)
            top = jnp.concatenate([first, jnp.zeros_like(first)], axis=1)
            bottom = jnp.concatenate([corner, second], axis=1)
            merged.append(jnp.concatenate([top, bottom], axis=0))
        inverses = merged
        size *= 2
    return inverses[0]


def lower_solve(strict_lower, right):
    rows_total = strict_lower.shape[0]
    tile = 128
    count = rows_total // tile
    if rows_total % tile or count & (count - 1):
        unit_lower = strict_lower + jnp.eye(rows_total, dtype=jnp.float32)
        return lax.linalg.triangular_solve(
            unit_lower, right, left_side=True, lower=True, unit_diagonal=True
        )
    return jnp.dot(unit_lower_inverse(strict_lower), right, precision=highest)


def shard_operators(query_block, key_block, vector_block, strength):
    block_rows = key_block.shape[0]
    head_width = key_block.shape[1]
    row_ids = jnp.arange(block_rows)
    strict = row_ids[:, None] > row_ids[None, :]
    causal = row_ids[:, None] >= row_ids[None, :]
    intersections = jnp.dot(vector_block, vector_block.T, precision=highest)
    strict_lower = jnp.where(strict, intersections * strength[None, :], 0.0)
    key_proj = jnp.where(strict, jnp.dot(vector_block, key_block.T, precision=highest), 0.0)
    solved = lower_solve(strict_lower, jnp.concatenate([key_proj, vector_block], axis=1))
    key_solve = solved[:, :block_rows]
    vector_solve = solved[:, block_rows:]
    weighted = strength[:, None] * vector_block
    keys_end = (key_block - jnp.dot(key_solve.T, weighted, precision=highest)).astype(jnp.bfloat16)
    transfer = jnp.eye(head_width, dtype=jnp.float32) - jnp.dot(
        vector_block.T, strength[:, None] * vector_solve, precision=highest
    )
    query_dots = jnp.where(causal, jnp.dot(query_block, vector_block.T, precision=highest), 0.0)
    scaled_dots = query_dots * strength[None, :]
    intra_scores = jnp.dot(query_block, key_block.T, precision=highest) - jnp.dot(
        scaled_dots, key_solve, precision=highest
    )
    rotated = query_block - jnp.dot(scaled_dots, vector_solve, precision=highest)
    return (intra_scores, keys_end, transfer, rotated)


def on_device(
    queries, key_states, value_states, transition_vectors, beta_logit, document_ids, out_weight
):
    block_rows = queries.shape[0]
    head_count = beta_logit.shape[1]
    head_width = queries.shape[1] // head_count
    score_scale = head_width ** (-0.5)

    def split_heads(flat):
        return jnp.transpose(flat.reshape(block_rows, head_count, head_width), (1, 0, 2))

    query_heads = split_heads(queries).astype(jnp.float32)
    key_heads = split_heads(key_states).astype(jnp.float32)
    value_heads = split_heads(value_states)
    vector_heads = split_heads(transition_vectors).astype(jnp.float32)
    value_columns = jnp.transpose(value_states.reshape(block_rows, head_count, head_width), (1, 2, 0))
    value_columns, vector_heads = lax.optimization_barrier((value_columns, vector_heads))
    unit_vectors = vector_heads / jnp.sqrt(
        jnp.sum(vector_heads * vector_heads, axis=2, keepdims=True) + epsilon
    )
    strength = 2.0 * jax.nn.sigmoid(beta_logit.T)
    every_value = lax.all_gather(value_columns, "ctx", axis=2, tiled=True)
    intra_scores, keys_end, transfer, rotated = jax.vmap(shard_operators)(
        query_heads, key_heads, unit_vectors, strength
    )
    every_value, keys_end = lax.optimization_barrier((every_value, keys_end))
    row_ids = jnp.arange(block_rows)
    causal = row_ids[:, None] >= row_ids[None, :]
    doc_float = (document_ids + 1).astype(jnp.float32)
    same_doc = doc_float[:, None] == doc_float[None, :]
    own_scores = jnp.where((causal & same_doc)[None], intra_scores * score_scale, masked_value)
    running_max = jnp.max(own_scores, axis=2)
    weights = jnp.exp(own_scores - running_max[..., None])
    running_sum = jnp.sum(weights, axis=2)
    accumulated = jnp.einsum(
        "hqk,hkd->hqd",
        weights.astype(jnp.bfloat16),
        value_heads,
        preferred_element_type=jnp.float32,
    )
    ctx_index = lax.axis_index("ctx")
    ctx_count = lax.axis_size("ctx")

    def attend(carried, key_pair, value_pair, transfer_in, key_docs):
        turned, running_max, running_sum, accumulated = carried
        scores = jnp.einsum(
            "hqd,hkd->hqk",
            turned.astype(jnp.bfloat16),
            key_pair,
            preferred_element_type=jnp.float32,
        )
        allowed = doc_float[:, None] == key_docs[None, :]
        scores = jnp.where(allowed[None], scores * score_scale, masked_value)
        new_max = jnp.maximum(running_max, jnp.max(scores, axis=2))
        factor = jnp.exp(running_max - new_max)
        weights = jnp.exp(scores - new_max[..., None])
        running_sum = running_sum * factor + jnp.sum(weights, axis=2)
        accumulated = accumulated * factor[..., None] + jnp.einsum(
            "hqk,hdk->hqd",
            weights.astype(jnp.bfloat16),
            value_pair,
            preferred_element_type=jnp.float32,
        )
        turned = jnp.einsum("hqd,hde->hqe", turned, transfer_in, precision=highest)
        return (turned, new_max, running_sum, accumulated)

    carried = (rotated, running_max, running_sum, accumulated)
    doc_rows = doc_float.reshape(-1, head_width)
    pad_rows = (-doc_rows.shape[0]) % 8
    doc_rows = jnp.concatenate([doc_rows, jnp.zeros((pad_rows, head_width), jnp.float32)], axis=0)
    meta_rows = jnp.concatenate(
        [transfer.reshape(head_count * head_width, head_width), doc_rows], axis=0
    ).astype(jnp.bfloat16)
    first_doc = doc_float[0]
    every_key = lax.all_gather(keys_end, "ctx", axis=1, tiled=True)
    is_live = jnp.bool_(True)
    steps = []
    for offset in range(1, ctx_count):
        pairs = [(s, s + offset) for s in range(ctx_count - offset)]
        meta_in = lax.ppermute(meta_rows, "ctx", pairs).astype(jnp.float32)
        transfer_in = meta_in[: head_count * head_width].reshape(head_count, head_width, head_width)
        key_docs = meta_in[head_count * head_width :].reshape(-1)[:block_rows]
        is_live = is_live & (ctx_index - offset >= 0) & (key_docs[block_rows - 1] == first_doc)
        steps.append((offset, transfer_in, key_docs, is_live))

    for offset, transfer_in, key_docs, step_live in steps:

        def take(inner, offset=offset, transfer_in=transfer_in, key_docs=key_docs):
            source = jnp.maximum(ctx_index - offset, 0)
            value_pair = lax.dynamic_slice_in_dim(every_value, source * block_rows, block_rows, 2)
            key_pair = lax.dynamic_slice_in_dim(every_key, source * block_rows, block_rows, 1)
            return attend(inner, key_pair, value_pair, transfer_in, key_docs)

        carried = lax.cond(step_live, take, lambda inner: inner, carried)
    attended = (carried[3] / carried[2][..., None]).astype(jnp.bfloat16)
    token_rows = jnp.transpose(attended, (1, 0, 2)).reshape(block_rows, head_count * head_width)
    return scatter_sum(token_rows, out_weight).astype(jnp.bfloat16)


def scatter_sum(token_rows, out_weight):
    head_count = lax.axis_size("head")
    if head_count % 2:
        projected = jnp.dot(token_rows, out_weight, preferred_element_type=jnp.float32)
        return lax.psum_scatter(projected, "head", scatter_dimension=0, tiled=True)
    chips = head_count // 2
    rows = token_rows.shape[0] // head_count
    head_index = lax.axis_index("head")
    core = head_index % 2
    chip = head_index // 2
    grouped = token_rows.reshape(chips, 2, rows, token_rows.shape[1])
    other = jnp.einsum(
        "crk,kf->crf",
        lax.dynamic_index_in_dim(grouped, 1 - core, 1, keepdims=False),
        out_weight,
        preferred_element_type=jnp.float32,
    )
    partner = [(h, h ^ 1) for h in range(head_count)]
    received = lax.ppermute(other.astype(jnp.bfloat16), "head", partner)
    mine = jnp.einsum(
        "crk,kf->crf",
        lax.dynamic_index_in_dim(grouped, core, 1, keepdims=False),
        out_weight,
        preferred_element_type=jnp.float32,
    )
    mine, received = lax.optimization_barrier((mine, received))
    chip_sum = mine + received.astype(jnp.float32)
    total = lax.dynamic_index_in_dim(chip_sum, chip, 0, keepdims=False)
    for shift in range(1, chips):
        pairs = [
            (2 * y + c, 2 * ((y + shift) % chips) + c) for y in range(chips) for c in range(2)
        ]
        outgoing = lax.dynamic_index_in_dim(chip_sum, (chip + shift) % chips, 0, keepdims=False)
        total = total + lax.ppermute(outgoing.astype(jnp.bfloat16), "head", pairs).astype(jnp.float32)
    return total


def solution(mesh):
    return jax.shard_map(
        on_device,
        mesh=mesh,
        in_specs=(
            P("ctx", "head"),
            P("ctx", "head"),
            P("ctx", "head"),
            P("ctx", "head"),
            P("ctx", "head"),
            P("ctx"),
            P("head", None),
        ),
        out_specs=P(("ctx", "head"), None),
        check_vma=False,
    )
```

```python
import jax
import jax.numpy as jnp
from jax import lax
from jax.sharding import PartitionSpec as P

epsilon = 1e-06
masked_value = -1e30
highest = lax.Precision.HIGHEST


def tile_inverse(tiles):
    width = tiles.shape[-1]
    row_ids = jnp.arange(width)[:, None]
    col_ids = jnp.arange(width)[None, :]
    identity = jnp.eye(width, dtype=jnp.float32)
    leaf_part = jnp.where((row_ids // 8) == (col_ids // 8), tiles, 0.0)
    square = jnp.matmul(leaf_part, leaf_part, precision=highest)
    fourth = jnp.matmul(square, square, precision=highest)
    inverse = jnp.matmul(identity - leaf_part, identity + square, precision=highest)
    inverse = jnp.matmul(inverse, identity + fourth, precision=highest)
    size = 8
    while size < width:
        pair_lower = (
            ((row_ids // (2 * size)) == (col_ids // (2 * size)))
            & ((row_ids // size) % 2 == 1)
            & ((col_ids // size) % 2 == 0)
        )
        corner = jnp.where(pair_lower, tiles, 0.0)
        inverse = inverse - jnp.matmul(
            inverse, jnp.matmul(corner, inverse, precision=highest), precision=highest
        )
        size *= 2
    return inverse


def unit_lower_inverse(strict_lower):
    rows_total = strict_lower.shape[0]
    tile = 128
    count = rows_total // tile
    blocks = [
        strict_lower[q * tile:(q + 1) * tile, q * tile:(q + 1) * tile][None] for q in range(count)
    ]
    inverses = list(tile_inverse(jnp.concatenate(blocks, axis=0)))
    size = tile
    while size < rows_total:
        merged = []
        for p in range(len(inverses) // 2):
            first = inverses[2 * p]
            second = inverses[2 * p + 1]
            start = 2 * p * size
            lower = strict_lower[start + size:start + 2 * size, start:start + size]
            corner = -jnp.dot(second, jnp.dot(lower, first, precision=highest), precision=highest)
            top = jnp.concatenate([first, jnp.zeros_like(first)], axis=1)
            bottom = jnp.concatenate([corner, second], axis=1)
            merged.append(jnp.concatenate([top, bottom], axis=0))
        inverses = merged
        size *= 2
    return inverses[0]


def lower_solve(strict_lower, right):
    rows_total = strict_lower.shape[0]
    tile = 128
    count = rows_total // tile
    if rows_total % tile or count & (count - 1):
        unit_lower = strict_lower + jnp.eye(rows_total, dtype=jnp.float32)
        return lax.linalg.triangular_solve(
            unit_lower, right, left_side=True, lower=True, unit_diagonal=True
        )
    return jnp.dot(unit_lower_inverse(strict_lower), right, precision=highest)


def shard_operators(query_block, key_block, vector_block, strength):
    block_rows = key_block.shape[0]
    head_width = key_block.shape[1]
    row_ids = jnp.arange(block_rows)
    strict = row_ids[:, None] > row_ids[None, :]
    causal = row_ids[:, None] >= row_ids[None, :]
    intersections = jnp.dot(vector_block, vector_block.T, precision=highest)
    strict_lower = jnp.where(strict, intersections * strength[None, :], 0.0)
    key_proj = jnp.where(strict, jnp.dot(vector_block, key_block.T, precision=highest), 0.0)
    solved = lower_solve(strict_lower, jnp.concatenate([key_proj, vector_block], axis=1))
    key_solve = solved[:, :block_rows]
    vector_solve = solved[:, block_rows:]
    weighted = strength[:, None] * vector_block
    keys_end = (key_block - jnp.dot(key_solve.T, weighted, precision=highest)).astype(jnp.bfloat16)
    transfer = jnp.eye(head_width, dtype=jnp.float32) - jnp.dot(
        vector_block.T, strength[:, None] * vector_solve, precision=highest
    )
    query_dots = jnp.where(causal, jnp.dot(query_block, vector_block.T, precision=highest), 0.0)
    scaled_dots = query_dots * strength[None, :]
    intra_scores = jnp.dot(query_block, key_block.T, precision=highest) - jnp.dot(
        scaled_dots, key_solve, precision=highest
    )
    rotated = query_block - jnp.dot(scaled_dots, vector_solve, precision=highest)
    return (intra_scores, keys_end, transfer, rotated)


def on_device(
    queries, key_states, value_states, transition_vectors, beta_logit, document_ids, out_weight
):
    block_rows = queries.shape[0]
    head_count = beta_logit.shape[1]
    head_width = queries.shape[1] // head_count
    score_scale = head_width ** (-0.5)

    def split_heads(flat):
        return jnp.transpose(flat.reshape(block_rows, head_count, head_width), (1, 0, 2))

    query_heads = split_heads(queries).astype(jnp.float32)
    key_heads = split_heads(key_states).astype(jnp.float32)
    value_heads = split_heads(value_states)
    vector_heads = split_heads(transition_vectors).astype(jnp.float32)
    value_columns = jnp.transpose(value_states.reshape(block_rows, head_count, head_width), (1, 2, 0))
    value_columns, vector_heads = lax.optimization_barrier((value_columns, vector_heads))
    unit_vectors = vector_heads / jnp.sqrt(
        jnp.sum(vector_heads * vector_heads, axis=2, keepdims=True) + epsilon
    )
    strength = 2.0 * jax.nn.sigmoid(beta_logit.T)
    every_value = lax.all_gather(value_columns, "ctx", axis=2, tiled=True)
    intra_scores, keys_end, transfer, rotated = jax.vmap(shard_operators)(
        query_heads, key_heads, unit_vectors, strength
    )
    every_value, rotated = lax.optimization_barrier((every_value, rotated))
    row_ids = jnp.arange(block_rows)
    causal = row_ids[:, None] >= row_ids[None, :]
    doc_float = (document_ids + 1).astype(jnp.float32)
    same_doc = doc_float[:, None] == doc_float[None, :]
    own_scores = jnp.where((causal & same_doc)[None], intra_scores * score_scale, masked_value)
    running_max = jnp.max(own_scores, axis=2)
    weights = jnp.exp(own_scores - running_max[..., None])
    running_sum = jnp.sum(weights, axis=2)
    accumulated = jnp.einsum(
        "hqk,hkd->hqd",
        weights.astype(jnp.bfloat16),
        value_heads,
        preferred_element_type=jnp.float32,
    )
    ctx_index = lax.axis_index("ctx")
    ctx_count = lax.axis_size("ctx")

    def attend(carried, key_pair, value_pair, transfer_in, key_docs):
        turned, running_max, running_sum, accumulated = carried
        scores = jnp.einsum(
            "hqd,hkd->hqk",
            turned.astype(jnp.bfloat16),
            key_pair,
            preferred_element_type=jnp.float32,
        )
        allowed = doc_float[:, None] == key_docs[None, :]
        scores = jnp.where(allowed[None], scores * score_scale, masked_value)
        new_max = jnp.maximum(running_max, jnp.max(scores, axis=2))
        factor = jnp.exp(running_max - new_max)
        weights = jnp.exp(scores - new_max[..., None])
        running_sum = running_sum * factor + jnp.sum(weights, axis=2)
        accumulated = accumulated * factor[..., None] + jnp.einsum(
            "hqk,hdk->hqd",
            weights.astype(jnp.bfloat16),
            value_pair,
            preferred_element_type=jnp.float32,
        )
        turned = jnp.einsum("hqd,hde->hqe", turned, transfer_in, precision=highest)
        return (turned, new_max, running_sum, accumulated)

    carried = (rotated, running_max, running_sum, accumulated)
    doc_rows = doc_float.reshape(-1, head_width)
    pad_rows = (-doc_rows.shape[0]) % 8
    doc_rows = jnp.concatenate([doc_rows, jnp.zeros((pad_rows, head_width), jnp.float32)], axis=0)
    meta_rows = jnp.concatenate(
        [transfer.reshape(head_count * head_width, head_width), doc_rows], axis=0
    ).astype(jnp.bfloat16)
    first_doc = doc_float[0]
    every_key = lax.all_gather(keys_end, "ctx", axis=1, tiled=True)
    is_live = jnp.bool_(True)
    steps = []
    for offset in range(1, ctx_count):
        pairs = [(s, s + offset) for s in range(ctx_count - offset)]
        meta_in = lax.ppermute(meta_rows, "ctx", pairs).astype(jnp.float32)
        transfer_in = meta_in[: head_count * head_width].reshape(head_count, head_width, head_width)
        key_docs = meta_in[head_count * head_width :].reshape(-1)[:block_rows]
        is_live = is_live & (ctx_index - offset >= 0) & (key_docs[block_rows - 1] == first_doc)
        steps.append((offset, transfer_in, key_docs, is_live))

    for offset, transfer_in, key_docs, step_live in steps:

        def take(inner, offset=offset, transfer_in=transfer_in, key_docs=key_docs):
            source = jnp.maximum(ctx_index - offset, 0)
            value_pair = lax.dynamic_slice_in_dim(every_value, source * block_rows, block_rows, 2)
            key_pair = lax.dynamic_slice_in_dim(every_key, source * block_rows, block_rows, 1)
            return attend(inner, key_pair, value_pair, transfer_in, key_docs)

        carried = lax.cond(step_live, take, lambda inner: inner, carried)
    attended = (carried[3] / carried[2][..., None]).astype(jnp.bfloat16)
    token_rows = jnp.transpose(attended, (1, 0, 2)).reshape(block_rows, head_count * head_width)
    return scatter_sum(token_rows, out_weight).astype(jnp.bfloat16)


def scatter_sum(token_rows, out_weight):
    head_count = lax.axis_size("head")
    if head_count % 2:
        projected = jnp.dot(token_rows, out_weight, preferred_element_type=jnp.float32)
        return lax.psum_scatter(projected, "head", scatter_dimension=0, tiled=True)
    chips = head_count // 2
    rows = token_rows.shape[0] // head_count
    head_index = lax.axis_index("head")
    core = head_index % 2
    chip = head_index // 2
    grouped = token_rows.reshape(chips, 2, rows, token_rows.shape[1])
    other = jnp.einsum(
        "crk,kf->crf",
        lax.dynamic_index_in_dim(grouped, 1 - core, 1, keepdims=False),
        out_weight,
        preferred_element_type=jnp.float32,
    )
    partner = [(h, h ^ 1) for h in range(head_count)]
    received = lax.ppermute(other.astype(jnp.bfloat16), "head", partner)
    mine = jnp.einsum(
        "crk,kf->crf",
        lax.dynamic_index_in_dim(grouped, core, 1, keepdims=False),
        out_weight,
        preferred_element_type=jnp.float32,
    )
    mine, received = lax.optimization_barrier((mine, received))
    chip_sum = mine + received.astype(jnp.float32)
    total = lax.dynamic_index_in_dim(chip_sum, chip, 0, keepdims=False)
    for shift in range(1, chips):
        pairs = [
            (2 * y + c, 2 * ((y + shift) % chips) + c) for y in range(chips) for c in range(2)
        ]
        outgoing = lax.dynamic_index_in_dim(chip_sum, (chip + shift) % chips, 0, keepdims=False)
        total = total + lax.ppermute(outgoing.astype(jnp.bfloat16), "head", pairs).astype(jnp.float32)
    return total


def solution(mesh):
    return jax.shard_map(
        on_device,
        mesh=mesh,
        in_specs=(
            P("ctx", "head"),
            P("ctx", "head"),
            P("ctx", "head"),
            P("ctx", "head"),
            P("ctx", "head"),
            P("ctx"),
            P("head", None),
        ),
        out_specs=P(("ctx", "head"), None),
        check_vma=False,
    )
```
